768 devices in a mesh: mem: 24 (over z_lo, x), lon: 32 (over z_hi, y, core).
Axes of the slice: x: 4, y: 8, z: 12 (z_hi: 2, z_lo: 6; z = z_hi * 6 + z_lo), core: 2. Of those that a mesh axis runs over, the one named last changes fastest.
Arguments:
- state: float32 [768, 32, 96, 128], P('mem', None, 'lon'), may hold values from -6 to 6
- courant: float32 [32, 96, 128], P(None, 'lon'), may hold values from -0.95 to 0.95
- weighting: float32 [32, 32], replicated, may hold values from -1 to 1
- bias_in: bfloat16 [48, 1024], replicated, may hold values from -0.875 to 0.875
- bias_offset: float32 [1024], replicated, may hold values from -3 to 3
- bias_out: bfloat16 [1024, 32], replicated, may hold values from -0.1875 to 0.1875
- predictors: bfloat16 [24, 32, 16, 16], P('mem', 'lon'), may hold values from -6 to 6
- obs_column: int32 [24, 32, 256], P('mem', 'lon'), may hold values from 0 to 15
- obs_channel: int32 [24, 32, 256], P('mem', 'lon'), may hold values from 0 to 31
- obs_value: float32 [24, 32, 256], P('mem', 'lon'), may hold values from -18 to 18
- obs_error: float32 [32], replicated, may hold values from 1 to 3
Outputs:
- analysis: float32 [768, 32, 96, 128], P('mem', None, 'lon')
The draws below stay inside these ranges and needn't reach their ends.
All inputs are finite; a program needn't handle non-finite values.
Results may differ from the reference program's by a relative error of at most 0.0014.
Values sent between devices are 32-bit elements; how exact they have to be, the bound alone decides.
No kernel may reach another device: no remote copies, remote signals or barrier semaphores. Data moves between devices by JAX's collectives and lax.ppermute only.
A program may use at most 64 MiB of HBM per device.

```python
import math
import jax
import jax.numpy as jnp
from jax import lax

MEMBERS = 768
LEV = 32
LAT = 128
NLON = 96
SECTORS = 32
NGROUP = 24
PATCH_COLS = 16
NPRED = 16
NIN = 48
HID = 1024
NCHAN = 32
NOBS = 256


def touch_ends(values, key, least, high):
    index_at = [jax.random.randint(jax.random.fold_in(key, axis), (), 0, length) for axis, length in enumerate(values.shape)]
    widest = values.shape.index(max(values.shape))
    beside = index_at[:widest] + [(index_at[widest] + 1) % values.shape[widest]] + index_at[widest + 1:]
    return values.at[tuple(index_at)].set(least).at[tuple(beside)].set(high)


def steps_of(key, shape, cuts, smallest, high):
    def one(dim, blocks):
        draws = jax.random.uniform(jax.random.fold_in(jax.random.fold_in(key, 6), dim), (blocks,), jnp.float32, smallest / len(cuts), high / len(cuts))
        return jnp.repeat(jnp.exp(draws), shape[dim] // blocks).reshape((-1,) + (1,) * (len(shape) - dim - 1))

    level = one(*cuts[0])
    for cut in cuts[1:]:
        level = level * one(*cut)
    return level


def bell_draw(stream_key, dims, scale, reach, pieces=(), kind=jnp.bfloat16):
    gain = steps_of(stream_key, dims, pieces, -0.22, 0.18) if pieces else 1.0
    entries = jax.random.normal(stream_key, dims, jnp.float32) * scale * gain
    return jnp.minimum(jnp.maximum(entries, -reach), reach).astype(kind)


def setup_inputs(seed: int = 0) -> dict:
    seeds = jax.random.split(jax.random.key(seed), 12)
    state = bell_draw(seeds[0], (MEMBERS, LEV, NLON, LAT), 1.0, 6.0, ((0, 24), (2, 32)), jnp.float32)
    courant = jnp.clip(jax.random.uniform(seeds[1], (LEV, NLON, LAT), jnp.float32, -0.95, 0.95) * steps_of(seeds[1], (LEV, NLON, LAT), ((1, 32),), -0.4, 0.0), -0.95, 0.95)
    weighting = bell_draw(seeds[2], (NCHAN, LEV), LEV ** -0.5, 1.0, (), jnp.float32)
    bias_in = bell_draw(seeds[3], (NIN, HID), NIN ** -0.5, 0.875)
    bias_offset = bell_draw(seeds[4], (HID,), 0.5, 3.0, (), jnp.float32)
    bias_out = bell_draw(seeds[5], (HID, NCHAN), HID ** -0.5, 0.1875)
    predictors = bell_draw(seeds[6], (NGROUP, SECTORS, PATCH_COLS, NPRED), 1.0, 6.0, ((0, 24), (1, 32)))
    obs_column = touch_ends(jax.random.randint(seeds[7], (NGROUP, SECTORS, NOBS), 0, PATCH_COLS), jax.random.fold_in(seeds[7], 1), 0, PATCH_COLS - 1).astype(jnp.int32)
    obs_channel = touch_ends(jax.random.randint(seeds[8], (NGROUP, SECTORS, NOBS), 0, NCHAN), jax.random.fold_in(seeds[8], 1), 0, NCHAN - 1).astype(jnp.int32)
    obs_value = bell_draw(seeds[9], (NGROUP, SECTORS, NOBS), 3.0, 18.0, ((0, 24), (1, 32)), jnp.float32)
    obs_error = jnp.clip(jnp.exp(jax.random.uniform(seeds[10], (NCHAN,), jnp.float32, math.log(1.0), math.log(3.0))), 1.0, 3.0)
    return dict(state=state, courant=courant, weighting=weighting, bias_in=bias_in, bias_offset=bias_offset, bias_out=bias_out, predictors=predictors, obs_column=obs_column, obs_channel=obs_channel, obs_value=obs_value, obs_error=obs_error)


highest = lax.Precision.HIGHEST

def chebyshev_root(low_end, high_end):
    points = [0.5 * (high_end + low_end) + 0.5 * (high_end - low_end) * math.cos(math.pi * (index + 0.5) / 4.0) for index in range(4)]
    coefficients = [0.0, 0.0, 0.0, 0.0]
    for index in range(4):
        basis_poly = [1.0]
        denominator = 1.0
        for other in range(4):
            if other != index:
                widened = [0.0] * (len(basis_poly) + 1)
                for power in range(len(basis_poly)):
                    widened[power + 1] += basis_poly[power]
                    widened[power] -= points[other] * basis_poly[power]
                basis_poly = widened
                denominator *= points[index] - points[other]
        factor = points[index] ** (-0.5) / denominator
        for power in range(4):
            coefficients[power] += factor * basis_poly[power]
    return tuple(coefficients)

def advect(field, courant):
    east = jnp.roll(field, -1, axis=2)
    west = jnp.roll(field, 1, axis=2)
    return field - 0.5 * courant * (east - west) + 0.5 * courant * courant * (east - 2.0 * field + west)

def apply_root(matrix, vectors):
    root_coefs = chebyshev_root(0.5, 12.0)
    result = root_coefs[3] * vectors
    for degree in (2, 1, 0):
        result = jnp.dot(matrix, result, precision=highest) + root_coefs[degree] * vectors
    return result

def analyse(patch_state, predictors, obs_column, obs_channel, obs_value, weighting, bias_in, bias_offset, bias_out, obs_error):
    members, levels, columns = patch_state.shape
    channels = weighting.shape[0]
    profile = jnp.transpose(patch_state, (0, 2, 1))
    phys = jnp.einsum('kcl,hl->kch', profile, weighting, precision=highest)
    extra = jnp.broadcast_to(predictors[None], (members, columns, predictors.shape[1]))
    net_in = jnp.concatenate([profile.astype(jnp.bfloat16), extra.astype(jnp.bfloat16)], axis=2)
    net_in = net_in.reshape(members * columns, net_in.shape[2])
    hidden = jnp.tanh(jnp.dot(net_in, bias_in, preferred_element_type=jnp.float32) + bias_offset).astype(jnp.bfloat16)
    evolved = phys + jnp.dot(hidden, bias_out, preferred_element_type=jnp.float32).reshape(members, columns, channels)
    table = evolved.reshape(members, columns * channels)
    picks = (obs_column * channels + obs_channel).astype(jnp.int32)
    hx = jnp.take(table, picks, axis=1)
    sigma = obs_error[obs_channel]
    hmean = lax.optimization_barrier(jnp.mean(hx, axis=0))
    root_count = math.sqrt(members - 1)
    spread = ((hx - hmean) / (sigma * root_count)).astype(jnp.bfloat16)
    innov = (obs_value - hmean) / sigma
    gram = jnp.dot(spread, spread.T, preferred_element_type=jnp.float32)
    spread_wide = spread.astype(jnp.float32)
    scale = 1.0 + jnp.sum(spread_wide * spread_wide) / members
    mtx = (jnp.eye(members, dtype=jnp.float32) + gram) / scale
    drive = jnp.dot(spread_wide, innov, precision=highest)
    mean_weights = apply_root(mtx, apply_root(mtx, drive)) / (scale * root_count)
    flat = patch_state.reshape(members, levels * columns)
    xmean = lax.optimization_barrier(jnp.mean(flat, axis=0))
    pert = flat - xmean
    spread_part = apply_root(mtx, pert)
    shift_part = jnp.dot(mean_weights, pert, precision=highest)
    result = xmean + spread_part / jnp.sqrt(scale) + shift_part
    return result.reshape(members, levels, columns)

def reference(state, courant, weighting, bias_in, bias_offset, bias_out, predictors, obs_column, obs_channel, obs_value, obs_error):
    field = advect(advect(state, courant), courant)
    members = field.shape[0]
    grouped = field.reshape(members, LEV, SECTORS, NGROUP, PATCH_COLS)
    patches = jnp.transpose(grouped, (3, 2, 0, 1, 4)).reshape(NGROUP * SECTORS, members, LEV, PATCH_COLS)
    pred_flat = predictors.reshape(NGROUP * SECTORS, PATCH_COLS, NPRED)
    column_flat = obs_column.reshape(NGROUP * SECTORS, NOBS)
    channel_flat = obs_channel.reshape(NGROUP * SECTORS, NOBS)
    value_flat = obs_value.reshape(NGROUP * SECTORS, NOBS)

    def one_patch(items):
        return analyse(items[0], items[1], items[2], items[3], items[4], weighting, bias_in, bias_offset, bias_out, obs_error)
    done = lax.map(one_patch, (patches, pred_flat, column_flat, channel_flat, value_flat))
    placed = jnp.transpose(done.reshape(NGROUP, SECTORS, members, LEV, PATCH_COLS), (2, 3, 1, 0, 4))
    placed = placed.reshape(members, LEV, NLON, LAT)
    return advect(advect(placed, courant), courant)
```

```python
import functools
import math

import jax
import jax.numpy as jnp
from jax import lax
from jax.experimental import pallas as pl
from jax.experimental.pallas import tpu as pltpu
from jax.sharding import PartitionSpec as P

highest = lax.Precision.HIGHEST


def chebyshev_root(low_end, high_end):
    points = [
        0.5 * (high_end + low_end)
        + 0.5 * (high_end - low_end) * math.cos(math.pi * (index + 0.5) / 4.0)
        for index in range(4)
    ]
    coefficients = [0.0, 0.0, 0.0, 0.0]
    for index in range(4):
        basis_poly = [1.0]
        denominator = 1.0
        for other in range(4):
            if other != index:
                widened = [0.0] * (len(basis_poly) + 1)
                for power in range(len(basis_poly)):
                    widened[power + 1] += basis_poly[power]
                    widened[power] -= points[other] * basis_poly[power]
                basis_poly = widened
                denominator *= points[index] - points[other]
        factor = points[index] ** (-0.5) / denominator
        for power in range(4):
            coefficients[power] += factor * basis_poly[power]
    return tuple(coefficients)


def ring_shift(block, axis, step):
    count = lax.axis_size(axis)
    pairs = [(i, (i + step) % count) for i in range(count)]
    return lax.ppermute(block, axis, pairs)


def advect_step(west, centre, east, courant):
    return (
        centre
        - 0.5 * courant * (east - west)
        + 0.5 * courant * courant * (east - 2.0 * centre + west)
    )


def two_passes(field, courant_padded):
    width = field.shape[1]
    from_left = ring_shift(field[:, width - 2 :], "lon", 1)
    from_right = ring_shift(field[:, :2], "lon", -1)
    padded = jnp.concatenate([from_left, field, from_right], axis=1)
    first = advect_step(
        padded[:, : width + 2], padded[:, 1 : width + 3], padded[:, 2 : width + 4], courant_padded
    )
    return advect_step(
        first[:, :width], first[:, 1 : width + 1], first[:, 2 : width + 2], courant_padded[1:-1]
    )


def apply_root(multiply, vectors):
    root_coefs = chebyshev_root(0.5, 12.0)
    result = root_coefs[3] * vectors
    for degree in (2, 1, 0):
        result = multiply(result) + root_coefs[degree] * vectors
    return result


def network_kernel(x_ref, w_in_ref, offset_ref, w_out_ref, out_ref):
    pre = jnp.dot(x_ref[...], w_in_ref[...], preferred_element_type=jnp.float32)
    hidden = jnp.tanh(pre + offset_ref[...]).astype(jnp.bfloat16)
    out_ref[...] = jnp.dot(hidden, w_out_ref[...], preferred_element_type=jnp.float32)


def network(net_in, bias_in, bias_offset, bias_out, rows=512):
    total, nin = net_in.shape
    hid = bias_in.shape[1]
    channels = bias_out.shape[1]
    return pl.pallas_call(
        network_kernel,
        out_shape=jax.ShapeDtypeStruct((total, channels), jnp.float32),
        grid=(total // rows,),
        in_specs=[
            pl.BlockSpec((rows, nin), lambda i: (i, 0)),
            pl.BlockSpec((nin, hid), lambda i: (0, 0)),
            pl.BlockSpec((1, hid), lambda i: (0, 0)),
            pl.BlockSpec((hid, channels), lambda i: (0, 0)),
        ],
        out_specs=pl.BlockSpec((rows, channels), lambda i: (i, 0)),
        cost_estimate=pl.CostEstimate(
            flops=2 * total * hid * (nin + channels),
            transcendentals=total * hid,
            bytes_accessed=total * (nin * 2 + channels * 4),
        ),
    )(net_in, bias_in, bias_offset.reshape(1, hid), bias_out)


def analyse(
    flat,
    predictors,
    obs_column,
    obs_channel,
    obs_value,
    weighting,
    bias_in,
    bias_offset,
    bias_out,
    obs_error,
    levels,
    columns,
):
    members = flat.shape[0]
    channels = weighting.shape[0]
    profile = jnp.transpose(flat.reshape(members, levels, columns), (0, 2, 1))
    rows = profile.reshape(members * columns, levels)
    phys = jnp.dot(rows, weighting.T, precision=highest)
    extra = jnp.broadcast_to(predictors[None], (members, columns, predictors.shape[1]))
    net_in = jnp.concatenate([profile.astype(jnp.bfloat16), extra], axis=2)
    net_in = net_in.reshape(members * columns, net_in.shape[2])
    evolved = phys + network(net_in, bias_in, bias_offset, bias_out)
    table = evolved.reshape(members, columns * channels)
    picks = obs_column * channels + obs_channel
    hx = jnp.take(table, picks, axis=1)
    onehot = (obs_channel[:, None] == jnp.arange(channels, dtype=jnp.int32)[None, :]).astype(
        jnp.float32
    )
    sigma = jnp.sum(onehot * obs_error[None, :], axis=1)
    hmean = jnp.mean(hx, axis=0)
    root_count = math.sqrt(members - 1)
    spread = ((hx - hmean) / (sigma * root_count)).astype(jnp.bfloat16)
    innov = (obs_value - hmean) / sigma
    spread_wide = spread.astype(jnp.float32)
    scale = 1.0 + jnp.sum(spread_wide * spread_wide) / members
    gram = jnp.dot(spread, spread.T, preferred_element_type=jnp.float32)
    mtx = (jnp.eye(members, dtype=jnp.float32) + gram) / scale

    def multiply(vectors):
        return jnp.dot(mtx, vectors, precision=highest)

    drive = jnp.dot(spread_wide, innov, precision=highest)
    mean_weights = apply_root(multiply, apply_root(multiply, drive)) / (scale * root_count)
    xmean = jnp.mean(flat, axis=0)
    pert = flat - xmean
    spread_part = apply_root(multiply, pert)
    shift_part = jnp.dot(mean_weights, pert, precision=highest)
    return xmean + spread_part / jnp.sqrt(scale) + shift_part


def shards(
    state,
    courant,
    weighting,
    bias_in,
    bias_offset,
    bias_out,
    predictors,
    obs_column,
    obs_channel,
    obs_value,
    obs_error,
):
    mem_local, levels, lon_local, lat_rows = state.shape
    groups = lax.axis_size("mem")
    patch_cols = lon_local * lat_rows // groups
    blocks = lat_rows // patch_cols
    field = jnp.transpose(state, (0, 2, 1, 3))
    wind = jnp.transpose(courant, (1, 0, 2))
    wind_padded = jnp.concatenate(
        [ring_shift(wind[-1:], "lon", 1), wind, ring_shift(wind[:1], "lon", -1)], axis=0
    )
    field = two_passes(field, wind_padded)
    outgoing = field.reshape(mem_local, lon_local, levels, blocks, patch_cols)
    outgoing = jnp.transpose(outgoing, (1, 3, 0, 2, 4)).reshape(
        groups, mem_local, levels * patch_cols
    )
    arrived = lax.all_to_all(outgoing, "mem", split_axis=0, concat_axis=0, tiled=True)
    flat = arrived.reshape(groups * mem_local, levels * patch_cols)
    analysed = analyse(
        flat,
        predictors[0, 0],
        obs_column[0, 0],
        obs_channel[0, 0],
        obs_value[0, 0],
        weighting,
        bias_in,
        bias_offset,
        bias_out,
        obs_error,
        levels,
        patch_cols,
    )
    returning = analysed.reshape(groups, mem_local, levels * patch_cols)
    restored = lax.all_to_all(returning, "mem", split_axis=0, concat_axis=0, tiled=True)
    restored = restored.reshape(lon_local, blocks, mem_local, levels, patch_cols)
    restored = jnp.transpose(restored, (2, 0, 3, 1, 4)).reshape(
        mem_local, lon_local, levels, lat_rows
    )
    field = two_passes(restored, wind_padded)
    return jnp.transpose(field, (0, 2, 1, 3))


def solution(mesh):
    placed = (
        P("mem", None, "lon", None),
        P(None, "lon", None),
        P(),
        P(),
        P(),
        P(),
        P("mem", "lon", None, None),
        P("mem", "lon", None),
        P("mem", "lon", None),
        P("mem", "lon", None),
        P(),
    )
    return jax.shard_map(
        shards, mesh=mesh, in_specs=placed, out_specs=P("mem", None, "lon", None), check_vma=False
    )
```

```python
import functools
import math

import jax
import jax.numpy as jnp
from jax import lax
from jax.experimental import pallas as pl
from jax.experimental.pallas import tpu as pltpu
from jax.sharding import PartitionSpec as P

highest = lax.Precision.HIGHEST


def chebyshev_root(low_end, high_end):
    points = [
        0.5 * (high_end + low_end)
        + 0.5 * (high_end - low_end) * math.cos(math.pi * (index + 0.5) / 4.0)
        for index in range(4)
    ]
    coefficients = [0.0, 0.0, 0.0, 0.0]
    for index in range(4):
        basis_poly = [1.0]
        denominator = 1.0
        for other in range(4):
            if other != index:
                widened = [0.0] * (len(basis_poly) + 1)
                for power in range(len(basis_poly)):
                    widened[power + 1] += basis_poly[power]
                    widened[power] -= points[other] * basis_poly[power]
                basis_poly = widened
                denominator *= points[index] - points[other]
        factor = points[index] ** (-0.5) / denominator
        for power in range(4):
            coefficients[power] += factor * basis_poly[power]
    return tuple(coefficients)


def ring_shift(block, axis, step):
    count = lax.axis_size(axis)
    pairs = [(i, (i + step) % count) for i in range(count)]
    return lax.ppermute(block, axis, pairs)


def advect_step(west, centre, east, courant):
    return (
        centre
        - 0.5 * courant * (east - west)
        + 0.5 * courant * courant * (east - 2.0 * centre + west)
    )


def halo_padded(field, from_left, from_right):
    return jnp.concatenate([from_left, field, from_right], axis=1)


def exchange(field, wind=None):
    mem_local, width, levels, lat_rows = field.shape
    to_right = field[:, width - 2 :].reshape(mem_local * 2, levels, lat_rows)
    to_left = field[:, :2].reshape(mem_local * 2, levels, lat_rows)
    if wind is not None:
        to_right = jnp.concatenate([to_right, wind[-1:]], axis=0)
        to_left = jnp.concatenate([to_left, wind[:1]], axis=0)
    got_left = ring_shift(to_right, "lon", 1)
    got_right = ring_shift(to_left, "lon", -1)
    count = mem_local * 2
    padded = halo_padded(
        field,
        got_left[:count].reshape(mem_local, 2, levels, lat_rows),
        got_right[:count].reshape(mem_local, 2, levels, lat_rows),
    )
    if wind is None:
        return padded, None
    return padded, jnp.concatenate([got_left[count:], wind, got_right[count:]], axis=0)


def two_passes(padded, courant_padded):
    width = padded.shape[1] - 4
    first = advect_step(
        padded[:, : width + 2], padded[:, 1 : width + 3], padded[:, 2 : width + 4], courant_padded
    )
    return advect_step(
        first[:, :width], first[:, 1 : width + 1], first[:, 2 : width + 2], courant_padded[1:-1]
    )


def apply_root(multiply, vectors):
    root_coefs = chebyshev_root(0.5, 12.0)
    result = root_coefs[3] * vectors
    for degree in (2, 1, 0):
        result = multiply(result) + root_coefs[degree] * vectors
    return result


def network_kernel(x_ref, pred_ref, w_prof_ref, w_pred_ref, offset_ref, w_out_ref, w_phys_ref, out_ref):
    x = x_ref[...]
    narrow = x.astype(jnp.bfloat16)
    extra = pred_ref[...]
    total = jnp.dot(x, w_phys_ref[...], precision=highest, preferred_element_type=jnp.float32)
    for part in range(w_prof_ref.shape[0]):
        pre = jnp.dot(narrow, w_prof_ref[part], preferred_element_type=jnp.float32)
        pre = pre + jnp.dot(extra, w_pred_ref[part], preferred_element_type=jnp.float32)
        hidden = jnp.tanh(pre + offset_ref[...]).astype(jnp.bfloat16)
        total = total + jnp.dot(hidden, w_out_ref[part], preferred_element_type=jnp.float32)
    out_ref[...] = total


def block_diagonal(matrix, parts, dtype):
    eye = jnp.eye(parts, dtype=dtype)
    rows, cols = matrix.shape
    return (eye[:, :, None, None] * matrix.astype(dtype)[None, None]).reshape(parts, parts * rows, cols)


def network(packed, predictors, weighting, bias_in, bias_offset, bias_out, levels, rows=256):
    total_rows, lanes = packed.shape
    parts = lanes // levels
    hid = bias_in.shape[1]
    channels = bias_out.shape[1]
    npred = predictors.shape[1]
    w_prof = block_diagonal(bias_in[:levels], parts, jnp.bfloat16)
    w_pred = block_diagonal(bias_in[levels:], parts, jnp.bfloat16)
    out_parts = block_diagonal(bias_out.T, parts, jnp.bfloat16)
    w_out = jnp.transpose(out_parts.reshape(parts, parts, channels, hid), (0, 3, 1, 2)).reshape(
        parts, hid, parts * channels
    )
    phys_parts = block_diagonal(weighting.T, parts, jnp.float32)
    w_phys = jnp.transpose(phys_parts, (1, 0, 2)).reshape(parts * levels, parts * channels)
    column_groups = predictors.shape[0] // parts
    pred_tiled = jnp.tile(
        predictors.reshape(column_groups, parts * npred), (rows // column_groups, 1)
    )
    const = lambda i: (0, 0)
    const3 = lambda i: (0, 0, 0)
    return pl.pallas_call(
        network_kernel,
        out_shape=jax.ShapeDtypeStruct((total_rows, parts * channels), jnp.float32),
        grid=(total_rows // rows,),
        in_specs=[
            pl.BlockSpec((rows, lanes), lambda i: (i, 0)),
            pl.BlockSpec((rows, parts * npred), const),
            pl.BlockSpec((parts, lanes, hid), const3),
            pl.BlockSpec((parts, parts * npred, hid), const3),
            pl.BlockSpec((1, hid), const),
            pl.BlockSpec((parts, hid, parts * channels), const3),
            pl.BlockSpec((lanes, parts * channels), const),
        ],
        out_specs=pl.BlockSpec((rows, parts * channels), lambda i: (i, 0)),
        cost_estimate=pl.CostEstimate(
            flops=2 * total_rows * parts * hid * (lanes + parts * npred + parts * channels),
            transcendentals=total_rows * parts * hid,
            bytes_accessed=total_rows * (lanes + parts * channels) * 4,
        ),
    )(packed, pred_tiled, w_prof, w_pred, bias_offset.reshape(1, hid), w_out, w_phys)


def analyse(
    flat,
    predictors,
    obs_column,
    obs_channel,
    obs_value,
    weighting,
    bias_in,
    bias_offset,
    bias_out,
    obs_error,
    levels,
    columns,
):
    members = flat.shape[0]
    channels = weighting.shape[0]
    packed = flat.reshape(members * columns * levels // 128, 128)
    evolved = network(packed, predictors, weighting, bias_in, bias_offset, bias_out, levels)
    table = evolved.reshape(members, columns * channels)
    picks = obs_column * channels + obs_channel
    hx = jnp.take(table, picks, axis=1)
    onehot = (obs_channel[:, None] == jnp.arange(channels, dtype=jnp.int32)[None, :]).astype(
        jnp.float32
    )
    sigma = jnp.sum(onehot * obs_error[None, :], axis=1)
    hmean = jnp.mean(hx, axis=0)
    root_count = math.sqrt(members - 1)
    spread = ((hx - hmean) / (sigma * root_count)).astype(jnp.bfloat16)
    innov = (obs_value - hmean) / sigma
    spread_wide = spread.astype(jnp.float32)
    scale = 1.0 + jnp.sum(spread_wide * spread_wide) / members
    gram = jnp.dot(spread, spread.T, preferred_element_type=jnp.float32)
    mtx = (jnp.eye(members, dtype=jnp.float32) + gram) / scale

    def multiply(vectors):
        return jnp.dot(mtx, vectors, precision=highest)

    def multiply_fast(vectors):
        return jnp.dot(mtx, vectors, precision=lax.Precision.HIGH)

    drive = jnp.dot(spread_wide, innov, precision=highest)
    mean_weights = apply_root(multiply, apply_root(multiply, drive)) / (scale * root_count)
    xmean = jnp.mean(flat, axis=0)
    pert = flat - xmean
    spread_part = apply_root(multiply_fast, pert)
    shift_part = jnp.dot(mean_weights, pert, precision=highest)
    return xmean + spread_part / jnp.sqrt(scale) + shift_part


def shards(
    state,
    courant,
    weighting,
    bias_in,
    bias_offset,
    bias_out,
    predictors,
    obs_column,
    obs_channel,
    obs_value,
    obs_error,
):
    mem_local, levels, lon_local, lat_rows = state.shape
    groups = lax.axis_size("mem")
    patch_cols = lon_local * lat_rows // groups
    blocks = lat_rows // patch_cols
    field = jnp.transpose(state, (0, 2, 1, 3))
    wind = jnp.transpose(courant, (1, 0, 2))
    padded, wind_padded = exchange(field, wind)
    field = two_passes(padded, wind_padded)
    outgoing = field.reshape(mem_local, lon_local, levels, blocks, patch_cols)
    outgoing = jnp.transpose(outgoing, (1, 3, 0, 4, 2)).reshape(
        groups, mem_local, patch_cols * levels
    )
    arrived = lax.all_to_all(outgoing, "mem", split_axis=0, concat_axis=0, tiled=True)
    flat = arrived.reshape(groups * mem_local, patch_cols * levels)
    analysed = analyse(
        flat,
        predictors[0, 0],
        obs_column[0, 0],
        obs_channel[0, 0],
        obs_value[0, 0],
        weighting,
        bias_in,
        bias_offset,
        bias_out,
        obs_error,
        levels,
        patch_cols,
    )
    returning = analysed.reshape(groups, mem_local, patch_cols * levels)
    restored = lax.all_to_all(returning, "mem", split_axis=0, concat_axis=0, tiled=True)
    restored = restored.reshape(lon_local, blocks, mem_local, patch_cols, levels)
    restored = jnp.transpose(restored, (2, 0, 4, 1, 3)).reshape(
        mem_local, lon_local, levels, lat_rows
    )
    padded, _ = exchange(restored)
    field = two_passes(padded, wind_padded)
    return jnp.transpose(field, (0, 2, 1, 3))


def solution(mesh):
    placed = (
        P("mem", None, "lon", None),
        P(None, "lon", None),
        P(),
        P(),
        P(),
        P(),
        P("mem", "lon", None, None),
        P("mem", "lon", None),
        P("mem", "lon", None),
        P("mem", "lon", None),
        P(),
    )
    return jax.shard_map(
        shards, mesh=mesh, in_specs=placed, out_specs=P("mem", None, "lon", None), check_vma=False
    )
```

```python
import functools
import math

import jax
import jax.numpy as jnp
from jax import lax
from jax.experimental import pallas as pl
from jax.experimental.pallas import tpu as pltpu
from jax.sharding import PartitionSpec as P

highest = lax.Precision.HIGHEST


def chebyshev_root(low_end, high_end):
    points = [
        0.5 * (high_end + low_end)
        + 0.5 * (high_end - low_end) * math.cos(math.pi * (index + 0.5) / 4.0)
        for index in range(4)
    ]
    coefficients = [0.0, 0.0, 0.0, 0.0]
    for index in range(4):
        basis_poly = [1.0]
        denominator = 1.0
        for other in range(4):
            if other != index:
                widened = [0.0] * (len(basis_poly) + 1)
                for power in range(len(basis_poly)):
                    widened[power + 1] += basis_poly[power]
                    widened[power] -= points[other] * basis_poly[power]
                basis_poly = widened
                denominator *= points[index] - points[other]
        factor = points[index] ** (-0.5) / denominator
        for power in range(4):
            coefficients[power] += factor * basis_poly[power]
    return tuple(coefficients)


def ring_shift(block, axis, step):
    count = lax.axis_size(axis)
    pairs = [(i, (i + step) % count) for i in range(count)]
    return lax.ppermute(block, axis, pairs)


def advect_step(west, centre, east, courant):
    return (
        centre
        - 0.5 * courant * (east - west)
        + 0.5 * courant * courant * (east - 2.0 * centre + west)
    )


def halo_padded(field, from_left, from_right):
    return jnp.concatenate([from_left, field, from_right], axis=1)


def exchange(field, wind=None):
    mem_local, width, levels, lat_rows = field.shape
    to_right = field[:, width - 2 :].reshape(mem_local * 2, levels, lat_rows)
    to_left = field[:, :2].reshape(mem_local * 2, levels, lat_rows)
    if wind is not None:
        to_right = jnp.concatenate([to_right, wind[-1:]], axis=0)
        to_left = jnp.concatenate([to_left, wind[:1]], axis=0)
    got_left = ring_shift(to_right, "lon", 1)
    got_right = ring_shift(to_left, "lon", -1)
    count = mem_local * 2
    padded = halo_padded(
        field,
        got_left[:count].reshape(mem_local, 2, levels, lat_rows),
        got_right[:count].reshape(mem_local, 2, levels, lat_rows),
    )
    if wind is None:
        return padded, None
    return padded, jnp.concatenate([got_left[count:], wind, got_right[count:]], axis=0)


def two_passes(padded, courant_padded):
    width = padded.shape[1] - 4
    first = advect_step(
        padded[:, : width + 2], padded[:, 1 : width + 3], padded[:, 2 : width + 4], courant_padded
    )
    return advect_step(
        first[:, :width], first[:, 1 : width + 1], first[:, 2 : width + 2], courant_padded[1:-1]
    )


def apply_root(multiply, vectors):
    root_coefs = chebyshev_root(0.5, 12.0)
    result = root_coefs[3] * vectors
    for degree in (2, 1, 0):
        result = multiply(result) + root_coefs[degree] * vectors
    return result


def network_kernel(x_ref, pred_ref, w_prof_ref, w_pred_ref, offset_ref, w_out_ref, w_phys_ref, out_ref):
    x = x_ref[...]
    narrow = x.astype(jnp.bfloat16)
    extra = pred_ref[...]
    total = jnp.dot(x, w_phys_ref[...], precision=highest, preferred_element_type=jnp.float32)
    for part in range(w_prof_ref.shape[0]):
        pre = jnp.dot(narrow, w_prof_ref[part], preferred_element_type=jnp.float32)
        pre = pre + jnp.dot(extra, w_pred_ref[part], preferred_element_type=jnp.float32)
        hidden = jnp.tanh(pre + offset_ref[...]).astype(jnp.bfloat16)
        total = total + jnp.dot(hidden, w_out_ref[part], preferred_element_type=jnp.float32)
    out_ref[...] = total


def block_diagonal(matrix, parts, dtype):
    eye = jnp.eye(parts, dtype=dtype)
    rows, cols = matrix.shape
    return (eye[:, :, None, None] * matrix.astype(dtype)[None, None]).reshape(parts, parts * rows, cols)


def network(packed, predictors, weighting, bias_in, bias_offset, bias_out, levels, rows=256):
    total_rows, lanes = packed.shape
    assert total_rows % rows == 0
    parts = lanes // levels
    hid = bias_in.shape[1]
    channels = bias_out.shape[1]
    npred = predictors.shape[1]
    w_prof = block_diagonal(bias_in[:levels], parts, jnp.bfloat16)
    w_pred = block_diagonal(bias_in[levels:], parts, jnp.bfloat16)
    out_parts = block_diagonal(bias_out.T, parts, jnp.bfloat16)
    w_out = jnp.transpose(out_parts.reshape(parts, parts, channels, hid), (0, 3, 1, 2)).reshape(
        parts, hid, parts * channels
    )
    phys_parts = block_diagonal(weighting.T, parts, jnp.float32)
    w_phys = jnp.transpose(phys_parts, (1, 0, 2)).reshape(parts * levels, parts * channels)
    column_groups = predictors.shape[0] // parts
    pred_tiled = jnp.tile(
        predictors.reshape(column_groups, parts * npred), (rows // column_groups, 1)
    )
    const = lambda i: (0, 0)
    const3 = lambda i: (0, 0, 0)
    return pl.pallas_call(
        network_kernel,
        out_shape=jax.ShapeDtypeStruct((total_rows, parts * channels), jnp.float32),
        grid=(total_rows // rows,),
        in_specs=[
            pl.BlockSpec((rows, lanes), lambda i: (i, 0)),
            pl.BlockSpec((rows, parts * npred), const),
            pl.BlockSpec((parts, lanes, hid), const3),
            pl.BlockSpec((parts, parts * npred, hid), const3),
            pl.BlockSpec((1, hid), const),
            pl.BlockSpec((parts, hid, parts * channels), const3),
            pl.BlockSpec((lanes, parts * channels), const),
        ],
        out_specs=pl.BlockSpec((rows, parts * channels), lambda i: (i, 0)),
        cost_estimate=pl.CostEstimate(
            flops=2 * total_rows * parts * hid * (lanes + parts * npred + parts * channels),
            transcendentals=total_rows * parts * hid,
            bytes_accessed=total_rows * (lanes + parts * channels) * 4,
        ),
    )(packed, pred_tiled, w_prof, w_pred, bias_offset.reshape(1, hid), w_out, w_phys)


def analyse(
    flats,
    predictors,
    obs_column,
    obs_channel,
    obs_value,
    weighting,
    bias_in,
    bias_offset,
    bias_out,
    obs_error,
    levels,
    columns,
):
    channels = weighting.shape[0]
    tables = []
    for part in flats:
        packed = part.reshape(part.shape[0] * columns * levels // 128, 128)
        evolved = network(packed, predictors, weighting, bias_in, bias_offset, bias_out, levels)
        tables.append(evolved.reshape(part.shape[0], columns * channels))
    table = jnp.concatenate(tables, axis=0)
    flat = jnp.concatenate(flats, axis=0)
    members = flat.shape[0]
    picks = obs_column * channels + obs_channel
    hx = jnp.take(table, picks, axis=1)
    onehot = (obs_channel[:, None] == jnp.arange(channels, dtype=jnp.int32)[None, :]).astype(
        jnp.float32
    )
    sigma = jnp.sum(onehot * obs_error[None, :], axis=1)
    hmean = jnp.mean(hx, axis=0)
    root_count = math.sqrt(members - 1)
    spread = ((hx - hmean) / (sigma * root_count)).astype(jnp.bfloat16)
    innov = (obs_value - hmean) / sigma
    spread_wide = spread.astype(jnp.float32)
    scale = 1.0 + jnp.sum(spread_wide * spread_wide) / members
    gram = jnp.dot(spread, spread.T, preferred_element_type=jnp.float32)
    mtx = (jnp.eye(members, dtype=jnp.float32) + gram) / scale

    def multiply_vector(vector):
        inner = jnp.sum(spread_wide * vector[:, None], axis=0)
        return (vector + jnp.sum(spread_wide * inner[None, :], axis=1)) / scale

    def multiply_fast(vectors):
        return jnp.dot(mtx, vectors, precision=lax.Precision.HIGH)

    drive = jnp.sum(spread_wide * innov[None, :], axis=1)
    mean_weights = apply_root(multiply_vector, apply_root(multiply_vector, drive)) / (
        scale * root_count
    )
    xmean = jnp.mean(flat, axis=0)
    pert = flat - xmean
    root_coefs = chebyshev_root(0.5, 12.0)
    result = root_coefs[3] * pert
    for degree in (2, 1):
        result = multiply_fast(result) + root_coefs[degree] * pert
    shift_part = jnp.dot(mean_weights, pert, precision=highest)
    root_scale = jnp.sqrt(scale)
    outs = []
    start = 0
    for part in flats:
        stop = start + part.shape[0]
        spread_part = (
            jnp.dot(mtx[start:stop], result, precision=lax.Precision.HIGH)
            + root_coefs[0] * pert[start:stop]
        )
        outs.append(xmean + spread_part / root_scale + shift_part)
        start = stop
    return outs


def shards(
    state,
    courant,
    weighting,
    bias_in,
    bias_offset,
    bias_out,
    predictors,
    obs_column,
    obs_channel,
    obs_value,
    obs_error,
):
    mem_local, levels, lon_local, lat_rows = state.shape
    groups = lax.axis_size("mem")
    patch_cols = lon_local * lat_rows // groups
    blocks = lat_rows // patch_cols
    halves = 2
    size = mem_local // halves
    field = jnp.transpose(state, (0, 2, 1, 3))
    wind = jnp.transpose(courant, (1, 0, 2))
    chunks = [field[h * size : (h + 1) * size] for h in range(halves)]
    first_padded, wind_padded = exchange(chunks[0], wind)
    paddeds = [first_padded] + [exchange(chunk)[0] for chunk in chunks[1:]]
    flats = []
    for padded in paddeds:
        forecast = two_passes(padded, wind_padded)
        outgoing = forecast.reshape(size, lon_local, levels, blocks, patch_cols)
        outgoing = jnp.transpose(outgoing, (1, 3, 0, 4, 2)).reshape(
            groups, size, patch_cols * levels
        )
        arrived = lax.all_to_all(outgoing, "mem", split_axis=0, concat_axis=0, tiled=True)
        flats.append(arrived.reshape(groups * size, patch_cols * levels))
    analysed = analyse(
        flats,
        predictors[0, 0],
        obs_column[0, 0],
        obs_channel[0, 0],
        obs_value[0, 0],
        weighting,
        bias_in,
        bias_offset,
        bias_out,
        obs_error,
        levels,
        patch_cols,
    )
    outs = []
    for part in analysed:
        returning = part.reshape(groups, size, patch_cols * levels)
        restored = lax.all_to_all(returning, "mem", split_axis=0, concat_axis=0, tiled=True)
        restored = restored.reshape(lon_local, blocks, size, patch_cols, levels)
        restored = jnp.transpose(restored, (2, 0, 4, 1, 3)).reshape(
            size, lon_local, levels, lat_rows
        )
        padded, _ = exchange(restored)
        outs.append(two_passes(padded, wind_padded))
    return jnp.transpose(jnp.concatenate(outs, axis=0), (0, 2, 1, 3))


def solution(mesh):
    placed = (
        P("mem", None, "lon", None),
        P(None, "lon", None),
        P(),
        P(),
        P(),
        P(),
        P("mem", "lon", None, None),
        P("mem", "lon", None),
        P("mem", "lon", None),
        P("mem", "lon", None),
        P(),
    )
    return jax.shard_map(
        shards, mesh=mesh, in_specs=placed, out_specs=P("mem", None, "lon", None), check_vma=False
    )
```

```python
import functools
import math

import jax
import jax.numpy as jnp
from jax import lax
from jax.experimental import pallas as pl
from jax.experimental.layout import Layout, with_layout_constraint
from jax.experimental.pallas import tpu as pltpu
from jax.sharding import PartitionSpec as P

highest = lax.Precision.HIGHEST


def chebyshev_root(low_end, high_end):
    points = [
        0.5 * (high_end + low_end)
        + 0.5 * (high_end - low_end) * math.cos(math.pi * (index + 0.5) / 4.0)
        for index in range(4)
    ]
    coefficients = [0.0, 0.0, 0.0, 0.0]
    for index in range(4):
        basis_poly = [1.0]
        denominator = 1.0
        for other in range(4):
            if other != index:
                widened = [0.0] * (len(basis_poly) + 1)
                for power in range(len(basis_poly)):
                    widened[power + 1] += basis_poly[power]
                    widened[power] -= points[other] * basis_poly[power]
                basis_poly = widened
                denominator *= points[index] - points[other]
        factor = points[index] ** (-0.5) / denominator
        for power in range(4):
            coefficients[power] += factor * basis_poly[power]
    return tuple(coefficients)


def ring_shift(block, axis, step):
    count = lax.axis_size(axis)
    pairs = [(i, (i + step) % count) for i in range(count)]
    return lax.ppermute(block, axis, pairs)


def advect_step(west, centre, east, courant):
    return (
        centre
        - 0.5 * courant * (east - west)
        + 0.5 * courant * courant * (east - 2.0 * centre + west)
    )


def halo_padded(field, from_left, from_right):
    return jnp.concatenate([from_left, field, from_right], axis=1)


def exchange(field, wind=None):
    mem_local, width, levels, lat_rows = field.shape
    to_right = field[:, width - 2 :].reshape(mem_local * 2, levels, lat_rows)
    to_left = field[:, :2].reshape(mem_local * 2, levels, lat_rows)
    if wind is not None:
        to_right = jnp.concatenate([to_right, wind[-1:]], axis=0)
        to_left = jnp.concatenate([to_left, wind[:1]], axis=0)
    got_left = ring_shift(to_right, "lon", 1)
    got_right = ring_shift(to_left, "lon", -1)
    count = mem_local * 2
    padded = halo_padded(
        field,
        got_left[:count].reshape(mem_local, 2, levels, lat_rows),
        got_right[:count].reshape(mem_local, 2, levels, lat_rows),
    )
    if wind is None:
        return padded, None
    return padded, jnp.concatenate([got_left[count:], wind, got_right[count:]], axis=0)


def two_passes(padded, courant_padded):
    width = padded.shape[1] - 4
    first = advect_step(
        padded[:, : width + 2], padded[:, 1 : width + 3], padded[:, 2 : width + 4], courant_padded
    )
    return advect_step(
        first[:, :width], first[:, 1 : width + 1], first[:, 2 : width + 2], courant_padded[1:-1]
    )


def apply_root(multiply, vectors):
    root_coefs = chebyshev_root(0.5, 12.0)
    result = root_coefs[3] * vectors
    for degree in (2, 1, 0):
        result = multiply(result) + root_coefs[degree] * vectors
    return result


def network_kernel(x_ref, pred_ref, w_prof_ref, w_pred_ref, offset_ref, w_out_ref, w_phys_ref, out_ref):
    x = x_ref[...]
    narrow = x.astype(jnp.bfloat16)
    extra = pred_ref[...]
    total = jnp.dot(x, w_phys_ref[...], precision=highest, preferred_element_type=jnp.float32)
    for part in range(w_prof_ref.shape[0]):
        pre = jnp.dot(narrow, w_prof_ref[part], preferred_element_type=jnp.float32)
        pre = pre + jnp.dot(extra, w_pred_ref[part], preferred_element_type=jnp.float32)
        hidden = jnp.tanh(pre + offset_ref[...]).astype(jnp.bfloat16)
        total = total + jnp.dot(hidden, w_out_ref[part], preferred_element_type=jnp.float32)
    out_ref[...] = total


def block_diagonal(matrix, parts, dtype):
    eye = jnp.eye(parts, dtype=dtype)
    rows, cols = matrix.shape
    return (eye[:, :, None, None] * matrix.astype(dtype)[None, None]).reshape(parts, parts * rows, cols)


def network(packed, predictors, weighting, bias_in, bias_offset, bias_out, levels, rows=256):
    total_rows, lanes = packed.shape
    assert total_rows % rows == 0
    parts = lanes // levels
    hid = bias_in.shape[1]
    channels = bias_out.shape[1]
    npred = predictors.shape[1]
    w_prof = block_diagonal(bias_in[:levels], parts, jnp.bfloat16)
    w_pred = block_diagonal(bias_in[levels:], parts, jnp.bfloat16)
    out_parts = block_diagonal(bias_out.T, parts, jnp.bfloat16)
    w_out = jnp.transpose(out_parts.reshape(parts, parts, channels, hid), (0, 3, 1, 2)).reshape(
        parts, hid, parts * channels
    )
    phys_parts = block_diagonal(weighting.T, parts, jnp.float32)
    w_phys = jnp.transpose(phys_parts, (1, 0, 2)).reshape(parts * levels, parts * channels)
    column_groups = predictors.shape[0] // parts
    pred_tiled = jnp.tile(
        predictors.reshape(column_groups, parts * npred), (rows // column_groups, 1)
    )
    const = lambda i: (0, 0)
    const3 = lambda i: (0, 0, 0)
    return pl.pallas_call(
        network_kernel,
        out_shape=jax.ShapeDtypeStruct((total_rows, parts * channels), jnp.float32),
        grid=(total_rows // rows,),
        in_specs=[
            pl.BlockSpec((rows, lanes), lambda i: (i, 0)),
            pl.BlockSpec((rows, parts * npred), const),
            pl.BlockSpec((parts, lanes, hid), const3),
            pl.BlockSpec((parts, parts * npred, hid), const3),
            pl.BlockSpec((1, hid), const),
            pl.BlockSpec((parts, hid, parts * channels), const3),
            pl.BlockSpec((lanes, parts * channels), const),
        ],
        out_specs=pl.BlockSpec((rows, parts * channels), lambda i: (i, 0)),
        cost_estimate=pl.CostEstimate(
            flops=2 * total_rows * parts * hid * (lanes + parts * npred + parts * channels),
            transcendentals=total_rows * parts * hid,
            bytes_accessed=total_rows * (lanes + parts * channels) * 4,
        ),
    )(packed, pred_tiled, w_prof, w_pred, bias_offset.reshape(1, hid), w_out, w_phys)


def analyse(
    flat,
    predictors,
    obs_column,
    obs_channel,
    obs_value,
    weighting,
    bias_in,
    bias_offset,
    bias_out,
    obs_error,
    levels,
    columns,
):
    members = flat.shape[0]
    channels = weighting.shape[0]
    packed = flat.reshape(members * columns * levels // 128, 128)
    evolved = network(packed, predictors, weighting, bias_in, bias_offset, bias_out, levels)
    table = evolved.reshape(members, columns * channels)
    picks = obs_column * channels + obs_channel
    hx = jnp.take(table, picks, axis=1)
    onehot = (obs_channel[:, None] == jnp.arange(channels, dtype=jnp.int32)[None, :]).astype(
        jnp.float32
    )
    sigma = jnp.sum(onehot * obs_error[None, :], axis=1)
    hmean = jnp.mean(hx, axis=0)
    root_count = math.sqrt(members - 1)
    spread = ((hx - hmean) / (sigma * root_count)).astype(jnp.bfloat16)
    innov = (obs_value - hmean) / sigma
    spread_wide = spread.astype(jnp.float32)
    scale = 1.0 + jnp.sum(spread_wide * spread_wide) / members
    gram = jnp.dot(spread, spread.T, preferred_element_type=jnp.float32)
    mtx = (jnp.eye(members, dtype=jnp.float32) + gram) / scale

    def multiply_vector(vector):
        inner = jnp.sum(spread_wide * vector[:, None], axis=0)
        return (vector + jnp.sum(spread_wide * inner[None, :], axis=1)) / scale

    def multiply_fast(vectors):
        return jnp.dot(mtx, vectors, precision=lax.Precision.HIGH)

    drive = jnp.dot(spread_wide, innov, precision=highest)
    mean_weights = apply_root(multiply_vector, apply_root(multiply_vector, drive)) / (
        scale * root_count
    )
    xmean = jnp.mean(flat, axis=0)
    pert = flat - xmean
    spread_part = apply_root(multiply_fast, pert)
    shift_part = jnp.dot(mean_weights, pert, precision=highest)
    return xmean + spread_part / jnp.sqrt(scale) + shift_part


def shards(
    state,
    courant,
    weighting,
    bias_in,
    bias_offset,
    bias_out,
    predictors,
    obs_column,
    obs_channel,
    obs_value,
    obs_error,
):
    mem_local, levels, lon_local, lat_rows = state.shape
    groups = lax.axis_size("mem")
    patch_cols = lon_local * lat_rows // groups
    blocks = lat_rows // patch_cols
    field = jnp.transpose(state, (0, 2, 1, 3))
    wind = jnp.transpose(courant, (1, 0, 2))
    padded, wind_padded = exchange(field, wind)
    field = two_passes(padded, wind_padded)
    outgoing = field.reshape(mem_local, lon_local, levels, blocks, patch_cols)
    outgoing = jnp.transpose(outgoing, (1, 3, 0, 4, 2)).reshape(
        groups, mem_local, patch_cols * levels
    )
    arrived = lax.all_to_all(outgoing, "mem", split_axis=0, concat_axis=0, tiled=True)
    flat = arrived.reshape(groups * mem_local, patch_cols * levels)
    analysed = analyse(
        flat,
        predictors[0, 0],
        obs_column[0, 0],
        obs_channel[0, 0],
        obs_value[0, 0],
        weighting,
        bias_in,
        bias_offset,
        bias_out,
        obs_error,
        levels,
        patch_cols,
    )
    returning = analysed.reshape(groups, mem_local, patch_cols * levels)
    restored = lax.all_to_all(returning, "mem", split_axis=0, concat_axis=0, tiled=True)
    restored = restored.reshape(lon_local, blocks, mem_local, patch_cols, levels)
    restored = jnp.transpose(restored, (2, 0, 4, 1, 3)).reshape(
        mem_local, lon_local, levels, lat_rows
    )
    restored = with_layout_constraint(restored, Layout((0, 1, 2, 3)))
    padded, _ = exchange(restored)
    field = two_passes(padded, wind_padded)
    return jnp.transpose(field, (0, 2, 1, 3))


def solution(mesh):
    placed = (
        P("mem", None, "lon", None),
        P(None, "lon", None),
        P(),
        P(),
        P(),
        P(),
        P("mem", "lon", None, None),
        P("mem", "lon", None),
        P("mem", "lon", None),
        P("mem", "lon", None),
        P(),
    )
    return jax.shard_map(
        shards, mesh=mesh, in_specs=placed, out_specs=P("mem", None, "lon", None), check_vma=False
    )
```

```python
import functools
import math

import jax
import jax.numpy as jnp
from jax import lax
from jax.experimental import pallas as pl
from jax.experimental.layout import Layout, with_layout_constraint
from jax.experimental.pallas import tpu as pltpu
from jax.sharding import PartitionSpec as P

highest = lax.Precision.HIGHEST


def chebyshev_root(low_end, high_end):
    points = [
        0.5 * (high_end + low_end)
        + 0.5 * (high_end - low_end) * math.cos(math.pi * (index + 0.5) / 4.0)
        for index in range(4)
    ]
    coefficients = [0.0, 0.0, 0.0, 0.0]
    for index in range(4):
        basis_poly = [1.0]
        denominator = 1.0
        for other in range(4):
            if other != index:
                widened = [0.0] * (len(basis_poly) + 1)
                for power in range(len(basis_poly)):
                    widened[power + 1] += basis_poly[power]
                    widened[power] -= points[other] * basis_poly[power]
                basis_poly = widened
                denominator *= points[index] - points[other]
        factor = points[index] ** (-0.5) / denominator
        for power in range(4):
            coefficients[power] += factor * basis_poly[power]
    return tuple(coefficients)


def ring_shift(block, axis, step):
    count = lax.axis_size(axis)
    pairs = [(i, (i + step) % count) for i in range(count)]
    return lax.ppermute(block, axis, pairs)


def advect_step(west, centre, east, courant):
    return (
        centre
        - 0.5 * courant * (east - west)
        + 0.5 * courant * courant * (east - 2.0 * centre + west)
    )


def halo_padded(field, from_left, from_right):
    return jnp.concatenate([from_left, field, from_right], axis=1)


def exchange(field, wind=None):
    mem_local, width, levels, lat_rows = field.shape
    to_right = field[:, width - 2 :].reshape(mem_local * 2, levels, lat_rows)
    to_left = field[:, :2].reshape(mem_local * 2, levels, lat_rows)
    if wind is not None:
        to_right = jnp.concatenate([to_right, wind[-1:]], axis=0)
        to_left = jnp.concatenate([to_left, wind[:1]], axis=0)
    got_left = ring_shift(to_right, "lon", 1)
    got_right = ring_shift(to_left, "lon", -1)
    count = mem_local * 2
    padded = halo_padded(
        field,
        got_left[:count].reshape(mem_local, 2, levels, lat_rows),
        got_right[:count].reshape(mem_local, 2, levels, lat_rows),
    )
    if wind is None:
        return padded, None
    return padded, jnp.concatenate([got_left[count:], wind, got_right[count:]], axis=0)


def two_passes(padded, courant_padded):
    width = padded.shape[1] - 4
    first = advect_step(
        padded[:, : width + 2], padded[:, 1 : width + 3], padded[:, 2 : width + 4], courant_padded
    )
    return advect_step(
        first[:, :width], first[:, 1 : width + 1], first[:, 2 : width + 2], courant_padded[1:-1]
    )


def apply_root(multiply, vectors):
    root_coefs = chebyshev_root(0.5, 12.0)
    result = root_coefs[3] * vectors
    for degree in (2, 1, 0):
        result = multiply(result) + root_coefs[degree] * vectors
    return result


def network_kernel(x_ref, pred_ref, w_prof_ref, w_pred_ref, offset_ref, w_out_ref, w_phys_ref, out_ref):
    x = x_ref[...]
    narrow = x.astype(jnp.bfloat16)
    extra = pred_ref[...]
    total = jnp.dot(x, w_phys_ref[...], precision=highest, preferred_element_type=jnp.float32)
    for part in range(w_prof_ref.shape[0]):
        pre = jnp.dot(narrow, w_prof_ref[part], preferred_element_type=jnp.float32)
        pre = pre + jnp.dot(extra, w_pred_ref[part], preferred_element_type=jnp.float32)
        hidden = jnp.tanh(pre + offset_ref[...]).astype(jnp.bfloat16)
        total = total + jnp.dot(hidden, w_out_ref[part], preferred_element_type=jnp.float32)
    out_ref[...] = total


def block_diagonal(matrix, parts, dtype):
    eye = jnp.eye(parts, dtype=dtype)
    rows, cols = matrix.shape
    return (eye[:, :, None, None] * matrix.astype(dtype)[None, None]).reshape(parts, parts * rows, cols)


def network(packed, predictors, weighting, bias_in, bias_offset, bias_out, levels, rows=256):
    total_rows, lanes = packed.shape
    assert total_rows % rows == 0
    parts = lanes // levels
    hid = bias_in.shape[1]
    channels = bias_out.shape[1]
    npred = predictors.shape[1]
    w_prof = block_diagonal(bias_in[:levels], parts, jnp.bfloat16)
    w_pred = block_diagonal(bias_in[levels:], parts, jnp.bfloat16)
    out_parts = block_diagonal(bias_out.T, parts, jnp.bfloat16)
    w_out = jnp.transpose(out_parts.reshape(parts, parts, channels, hid), (0, 3, 1, 2)).reshape(
        parts, hid, parts * channels
    )
    phys_parts = block_diagonal(weighting.T, parts, jnp.float32)
    w_phys = jnp.transpose(phys_parts, (1, 0, 2)).reshape(parts * levels, parts * channels)
    column_groups = predictors.shape[0] // parts
    pred_tiled = jnp.tile(
        predictors.reshape(column_groups, parts * npred), (rows // column_groups, 1)
    )
    const = lambda i: (0, 0)
    const3 = lambda i: (0, 0, 0)
    return pl.pallas_call(
        network_kernel,
        out_shape=jax.ShapeDtypeStruct((total_rows, parts * channels), jnp.float32),
        grid=(total_rows // rows,),
        in_specs=[
            pl.BlockSpec((rows, lanes), lambda i: (i, 0)),
            pl.BlockSpec((rows, parts * npred), const),
            pl.BlockSpec((parts, lanes, hid), const3),
            pl.BlockSpec((parts, parts * npred, hid), const3),
            pl.BlockSpec((1, hid), const),
            pl.BlockSpec((parts, hid, parts * channels), const3),
            pl.BlockSpec((lanes, parts * channels), const),
        ],
        out_specs=pl.BlockSpec((rows, parts * channels), lambda i: (i, 0)),
        cost_estimate=pl.CostEstimate(
            flops=2 * total_rows * parts * hid * (lanes + parts * npred + parts * channels),
            transcendentals=total_rows * parts * hid,
            bytes_accessed=total_rows * (lanes + parts * channels) * 4,
        ),
    )(packed, pred_tiled, w_prof, w_pred, bias_offset.reshape(1, hid), w_out, w_phys)


def mean_weight_kernel(root_count, spread_ref, drive_ref, scale_ref, out_ref):
    spread = spread_ref[...]
    scale = scale_ref[...]

    def multiply(vector):
        inner = jnp.sum(spread * vector, axis=0, keepdims=True)
        return (vector + jnp.sum(spread * inner, axis=1, keepdims=True)) / scale

    out_ref[...] = apply_root(multiply, apply_root(multiply, drive_ref[...])) / (scale * root_count)


def mean_weight_chain(spread_wide, drive, scale, root_count):
    members, obs = spread_wide.shape
    out = pl.pallas_call(
        functools.partial(mean_weight_kernel, root_count),
        out_shape=jax.ShapeDtypeStruct((members, 1), jnp.float32),
        cost_estimate=pl.CostEstimate(
            flops=24 * members * obs, transcendentals=0, bytes_accessed=members * obs * 4
        ),
    )(spread_wide, drive.reshape(members, 1), scale.reshape(1, 1))
    return out[:, 0]


def analyse(
    flat,
    predictors,
    obs_column,
    obs_channel,
    obs_value,
    weighting,
    bias_in,
    bias_offset,
    bias_out,
    obs_error,
    levels,
    columns,
):
    members = flat.shape[0]
    channels = weighting.shape[0]
    packed = flat.reshape(members * columns * levels // 128, 128)
    evolved = network(packed, predictors, weighting, bias_in, bias_offset, bias_out, levels)
    table = evolved.reshape(members, columns * channels)
    picks = obs_column * channels + obs_channel
    hx = jnp.take(table, picks, axis=1)
    onehot = (obs_channel[:, None] == jnp.arange(channels, dtype=jnp.int32)[None, :]).astype(
        jnp.float32
    )
    sigma = jnp.sum(onehot * obs_error[None, :], axis=1)
    hmean = jnp.mean(hx, axis=0)
    root_count = math.sqrt(members - 1)
    spread = ((hx - hmean) / (sigma * root_count)).astype(jnp.bfloat16)
    innov = (obs_value - hmean) / sigma
    spread_wide = spread.astype(jnp.float32)
    scale = 1.0 + jnp.sum(spread_wide * spread_wide) / members
    gram = jnp.dot(spread, spread.T, preferred_element_type=jnp.float32)
    mtx = (jnp.eye(members, dtype=jnp.float32) + gram) / scale

    def multiply_fast(vectors):
        return jnp.dot(mtx, vectors, precision=lax.Precision.HIGH)

    drive = jnp.dot(spread_wide, innov, precision=highest)
    mean_weights = mean_weight_chain(spread_wide, drive, scale, root_count)
    xmean = jnp.mean(flat, axis=0)
    pert = flat - xmean
    spread_part = apply_root(multiply_fast, pert)
    shift_part = jnp.dot(mean_weights, pert, precision=highest)
    return xmean + spread_part / jnp.sqrt(scale) + shift_part


def shards(
    state,
    courant,
    weighting,
    bias_in,
    bias_offset,
    bias_out,
    predictors,
    obs_column,
    obs_channel,
    obs_value,
    obs_error,
):
    mem_local, levels, lon_local, lat_rows = state.shape
    groups = lax.axis_size("mem")
    patch_cols = lon_local * lat_rows // groups
    blocks = lat_rows // patch_cols
    field = jnp.transpose(state, (0, 2, 1, 3))
    wind = jnp.transpose(courant, (1, 0, 2))
    padded, wind_padded = exchange(field, wind)
    field = two_passes(padded, wind_padded)
    outgoing = field.reshape(mem_local, lon_local, levels, blocks, patch_cols)
    outgoing = jnp.transpose(outgoing, (1, 3, 0, 4, 2)).reshape(
        groups, mem_local, patch_cols * levels
    )
    arrived = lax.all_to_all(outgoing, "mem", split_axis=0, concat_axis=0, tiled=True)
    flat = arrived.reshape(groups * mem_local, patch_cols * levels)
    analysed = analyse(
        flat,
        predictors[0, 0],
        obs_column[0, 0],
        obs_channel[0, 0],
        obs_value[0, 0],
        weighting,
        bias_in,
        bias_offset,
        bias_out,
        obs_error,
        levels,
        patch_cols,
    )
    returning = analysed.reshape(groups, mem_local, patch_cols * levels)
    restored = lax.all_to_all(returning, "mem", split_axis=0, concat_axis=0, tiled=True)
    restored = restored.reshape(lon_local, blocks, mem_local, patch_cols, levels)
    restored = jnp.transpose(restored, (2, 0, 4, 1, 3)).reshape(
        mem_local, lon_local, levels, lat_rows
    )
    restored = with_layout_constraint(restored, Layout((0, 1, 2, 3)))
    padded, _ = exchange(restored)
    field = two_passes(padded, wind_padded)
    return jnp.transpose(field, (0, 2, 1, 3))


def solution(mesh):
    placed = (
        P("mem", None, "lon", None),
        P(None, "lon", None),
        P(),
        P(),
        P(),
        P(),
        P("mem", "lon", None, None),
        P("mem", "lon", None),
        P("mem", "lon", None),
        P("mem", "lon", None),
        P(),
    )
    return jax.shard_map(
        shards, mesh=mesh, in_specs=placed, out_specs=P("mem", None, "lon", None), check_vma=False
    )
```

```python
import functools
import math

import jax
import jax.numpy as jnp
from jax import lax
from jax.experimental import pallas as pl
from jax.experimental.layout import Layout, with_layout_constraint
from jax.experimental.pallas import tpu as pltpu
from jax.sharding import PartitionSpec as P

highest = lax.Precision.HIGHEST


def chebyshev_root(low_end, high_end):
    points = [
        0.5 * (high_end + low_end)
        + 0.5 * (high_end - low_end) * math.cos(math.pi * (index + 0.5) / 4.0)
        for index in range(4)
    ]
    coefficients = [0.0, 0.0, 0.0, 0.0]
    for index in range(4):
        basis_poly = [1.0]
        denominator = 1.0
        for other in range(4):
            if other != index:
                widened = [0.0] * (len(basis_poly) + 1)
                for power in range(len(basis_poly)):
                    widened[power + 1] += basis_poly[power]
                    widened[power] -= points[other] * basis_poly[power]
                basis_poly = widened
                denominator *= points[index] - points[other]
        factor = points[index] ** (-0.5) / denominator
        for power in range(4):
            coefficients[power] += factor * basis_poly[power]
    return tuple(coefficients)


def ring_shift(block, axis, step):
    count = lax.axis_size(axis)
    pairs = [(i, (i + step) % count) for i in range(count)]
    return lax.ppermute(block, axis, pairs)


def advect_step(west, centre, east, courant):
    return (
        centre
        - 0.5 * courant * (east - west)
        + 0.5 * courant * courant * (east - 2.0 * centre + west)
    )


def halo_padded(field, from_left, from_right):
    return jnp.concatenate([from_left, field, from_right], axis=1)


def exchange(field, wind=None):
    mem_local, width, levels, lat_rows = field.shape
    to_right = field[:, width - 2 :].reshape(mem_local * 2, levels, lat_rows)
    to_left = field[:, :2].reshape(mem_local * 2, levels, lat_rows)
    if wind is not None:
        to_right = jnp.concatenate([to_right, wind[-1:]], axis=0)
        to_left = jnp.concatenate([to_left, wind[:1]], axis=0)
    got_left = ring_shift(to_right, "lon", 1)
    got_right = ring_shift(to_left, "lon", -1)
    count = mem_local * 2
    padded = halo_padded(
        field,
        got_left[:count].reshape(mem_local, 2, levels, lat_rows),
        got_right[:count].reshape(mem_local, 2, levels, lat_rows),
    )
    if wind is None:
        return padded, None
    return padded, jnp.concatenate([got_left[count:], wind, got_right[count:]], axis=0)


def two_passes(padded, courant_padded):
    width = padded.shape[1] - 4
    first = advect_step(
        padded[:, : width + 2], padded[:, 1 : width + 3], padded[:, 2 : width + 4], courant_padded
    )
    return advect_step(
        first[:, :width], first[:, 1 : width + 1], first[:, 2 : width + 2], courant_padded[1:-1]
    )


def apply_root(multiply, vectors):
    root_coefs = chebyshev_root(0.5, 12.0)
    result = root_coefs[3] * vectors
    for degree in (2, 1, 0):
        result = multiply(result) + root_coefs[degree] * vectors
    return result


def network_kernel(x_ref, pred_ref, w_prof_ref, w_pred_ref, offset_ref, w_out_ref, w_phys_ref, out_ref):
    x = x_ref[...]
    narrow = x.astype(jnp.bfloat16)
    extra = pred_ref[...]
    total = jnp.dot(x, w_phys_ref[...], precision=highest, preferred_element_type=jnp.float32)
    for part in range(w_prof_ref.shape[0]):
        pre = jnp.dot(narrow, w_prof_ref[part], preferred_element_type=jnp.float32)
        pre = pre + jnp.dot(extra, w_pred_ref[part], preferred_element_type=jnp.float32)
        hidden = jnp.tanh(pre + offset_ref[...]).astype(jnp.bfloat16)
        total = total + jnp.dot(hidden, w_out_ref[part], preferred_element_type=jnp.float32)
    out_ref[...] = total


def block_diagonal(matrix, parts, dtype):
    eye = jnp.eye(parts, dtype=dtype)
    rows, cols = matrix.shape
    return (eye[:, :, None, None] * matrix.astype(dtype)[None, None]).reshape(parts, parts * rows, cols)


def network(packed, predictors, weighting, bias_in, bias_offset, bias_out, levels, rows=256):
    total_rows, lanes = packed.shape
    assert total_rows % rows == 0
    parts = lanes // levels
    hid = bias_in.shape[1]
    channels = bias_out.shape[1]
    npred = predictors.shape[1]
    w_prof = block_diagonal(bias_in[:levels], parts, jnp.bfloat16)
    w_pred = block_diagonal(bias_in[levels:], parts, jnp.bfloat16)
    out_parts = block_diagonal(bias_out.T, parts, jnp.bfloat16)
    w_out = jnp.transpose(out_parts.reshape(parts, parts, channels, hid), (0, 3, 1, 2)).reshape(
        parts, hid, parts * channels
    )
    phys_parts = block_diagonal(weighting.T, parts, jnp.float32)
    w_phys = jnp.transpose(phys_parts, (1, 0, 2)).reshape(parts * levels, parts * channels)
    column_groups = predictors.shape[0] // parts
    pred_tiled = jnp.tile(
        predictors.reshape(column_groups, parts * npred), (rows // column_groups, 1)
    )
    const = lambda i: (0, 0)
    const3 = lambda i: (0, 0, 0)
    return pl.pallas_call(
        network_kernel,
        out_shape=jax.ShapeDtypeStruct((total_rows, parts * channels), jnp.float32),
        grid=(total_rows // rows,),
        in_specs=[
            pl.BlockSpec((rows, lanes), lambda i: (i, 0)),
            pl.BlockSpec((rows, parts * npred), const),
            pl.BlockSpec((parts, lanes, hid), const3),
            pl.BlockSpec((parts, parts * npred, hid), const3),
            pl.BlockSpec((1, hid), const),
            pl.BlockSpec((parts, hid, parts * channels), const3),
            pl.BlockSpec((lanes, parts * channels), const),
        ],
        out_specs=pl.BlockSpec((rows, parts * channels), lambda i: (i, 0)),
        cost_estimate=pl.CostEstimate(
            flops=2 * total_rows * parts * hid * (lanes + parts * npred + parts * channels),
            transcendentals=total_rows * parts * hid,
            bytes_accessed=total_rows * (lanes + parts * channels) * 4,
        ),
    )(packed, pred_tiled, w_prof, w_pred, bias_offset.reshape(1, hid), w_out, w_phys)


def analyse(
    flat,
    predictors,
    obs_column,
    obs_channel,
    obs_value,
    weighting,
    bias_in,
    bias_offset,
    bias_out,
    obs_error,
    levels,
    columns,
):
    members = flat.shape[0]
    channels = weighting.shape[0]
    packed = flat.reshape(members * columns * levels // 128, 128)
    evolved = network(packed, predictors, weighting, bias_in, bias_offset, bias_out, levels)
    table = evolved.reshape(members, columns * channels)
    picks = obs_column * channels + obs_channel
    hx = jnp.take(table, picks, axis=1)
    onehot = (obs_channel[:, None] == jnp.arange(channels, dtype=jnp.int32)[None, :]).astype(
        jnp.float32
    )
    sigma = jnp.sum(onehot * obs_error[None, :], axis=1)
    hmean = jnp.mean(hx, axis=0)
    root_count = math.sqrt(members - 1)
    spread = ((hx - hmean) / (sigma * root_count)).astype(jnp.bfloat16)
    innov = (obs_value - hmean) / sigma
    spread_wide = spread.astype(jnp.float32)
    scale = 1.0 + jnp.sum(spread_wide * spread_wide) / members
    gram = jnp.dot(spread, spread.T, preferred_element_type=jnp.float32)
    mtx = (jnp.eye(members, dtype=jnp.float32) + gram) / scale

    def multiply(vectors):
        return jnp.dot(mtx, vectors, precision=highest)

    def multiply_fast(vectors):
        return jnp.dot(mtx, vectors, precision=lax.Precision.HIGH)

    drive = jnp.dot(spread_wide, innov, precision=highest)
    mean_weights = apply_root(multiply, apply_root(multiply, drive)) / (scale * root_count)
    xmean = jnp.mean(flat, axis=0)
    pert = flat - xmean
    spread_part = apply_root(multiply_fast, pert)
    shift_part = jnp.dot(mean_weights, pert, precision=highest)
    return xmean + spread_part / jnp.sqrt(scale) + shift_part


def shards(
    state,
    courant,
    weighting,
    bias_in,
    bias_offset,
    bias_out,
    predictors,
    obs_column,
    obs_channel,
    obs_value,
    obs_error,
):
    mem_local, levels, lon_local, lat_rows = state.shape
    groups = lax.axis_size("mem")
    patch_cols = lon_local * lat_rows // groups
    blocks = lat_rows // patch_cols
    field = jnp.transpose(state, (0, 2, 1, 3))
    wind = jnp.transpose(courant, (1, 0, 2))
    padded, wind_padded = exchange(field, wind)
    field = two_passes(padded, wind_padded)
    outgoing = field.reshape(mem_local, lon_local, levels, blocks, patch_cols)
    outgoing = jnp.transpose(outgoing, (1, 3, 0, 4, 2)).reshape(
        groups, mem_local, patch_cols * levels
    )
    arrived = lax.all_to_all(outgoing, "mem", split_axis=0, concat_axis=0, tiled=True)
    flat = arrived.reshape(groups * mem_local, patch_cols * levels)
    analysed = analyse(
        flat,
        predictors[0, 0],
        obs_column[0, 0],
        obs_channel[0, 0],
        obs_value[0, 0],
        weighting,
        bias_in,
        bias_offset,
        bias_out,
        obs_error,
        levels,
        patch_cols,
    )
    returning = analysed.reshape(groups, mem_local, patch_cols * levels)
    restored = lax.all_to_all(returning, "mem", split_axis=0, concat_axis=0, tiled=True)
    restored = restored.reshape(lon_local, blocks, mem_local, patch_cols, levels)
    restored = jnp.transpose(restored, (2, 0, 4, 1, 3)).reshape(
        mem_local, lon_local, levels, lat_rows
    )
    restored = with_layout_constraint(restored, Layout((0, 1, 2, 3)))
    padded, _ = exchange(restored)
    field = two_passes(padded, wind_padded)
    return jnp.transpose(field, (0, 2, 1, 3))


def solution(mesh):
    placed = (
        P("mem", None, "lon", None),
        P(None, "lon", None),
        P(),
        P(),
        P(),
        P(),
        P("mem", "lon", None, None),
        P("mem", "lon", None),
        P("mem", "lon", None),
        P("mem", "lon", None),
        P(),
    )
    return jax.shard_map(
        shards, mesh=mesh, in_specs=placed, out_specs=P("mem", None, "lon", None), check_vma=False
    )
```

```python
import functools
import math

import jax
import jax.numpy as jnp
from jax import lax
from jax.experimental import pallas as pl
from jax.experimental.layout import Layout, with_layout_constraint
from jax.experimental.pallas import tpu as pltpu
from jax.sharding import PartitionSpec as P

highest = lax.Precision.HIGHEST


def chebyshev_root(low_end, high_end):
    points = [
        0.5 * (high_end + low_end)
        + 0.5 * (high_end - low_end) * math.cos(math.pi * (index + 0.5) / 4.0)
        for index in range(4)
    ]
    coefficients = [0.0, 0.0, 0.0, 0.0]
    for index in range(4):
        basis_poly = [1.0]
        denominator = 1.0
        for other in range(4):
            if other != index:
                widened = [0.0] * (len(basis_poly) + 1)
                for power in range(len(basis_poly)):
                    widened[power + 1] += basis_poly[power]
                    widened[power] -= points[other] * basis_poly[power]
                basis_poly = widened
                denominator *= points[index] - points[other]
        factor = points[index] ** (-0.5) / denominator
        for power in range(4):
            coefficients[power] += factor * basis_poly[power]
    return tuple(coefficients)


def ring_shift(block, axis, step):
    count = lax.axis_size(axis)
    pairs = [(i, (i + step) % count) for i in range(count)]
    return lax.ppermute(block, axis, pairs)


def advect_step(west, centre, east, courant):
    return (
        centre
        - 0.5 * courant * (east - west)
        + 0.5 * courant * courant * (east - 2.0 * centre + west)
    )


def halo_padded(field, from_left, from_right):
    return jnp.concatenate([from_left, field, from_right], axis=1)


def exchange(field, wind=None):
    mem_local, width, levels, lat_rows = field.shape
    to_right = field[:, width - 2 :].reshape(mem_local * 2, levels, lat_rows)
    to_left = field[:, :2].reshape(mem_local * 2, levels, lat_rows)
    if wind is not None:
        to_right = jnp.concatenate([to_right, wind[-1:]], axis=0)
        to_left = jnp.concatenate([to_left, wind[:1]], axis=0)
    got_left = ring_shift(to_right, "lon", 1)
    got_right = ring_shift(to_left, "lon", -1)
    count = mem_local * 2
    padded = halo_padded(
        field,
        got_left[:count].reshape(mem_local, 2, levels, lat_rows),
        got_right[:count].reshape(mem_local, 2, levels, lat_rows),
    )
    if wind is None:
        return padded, None
    return padded, jnp.concatenate([got_left[count:], wind, got_right[count:]], axis=0)


def two_passes(padded, courant_padded):
    width = padded.shape[1] - 4
    first = advect_step(
        padded[:, : width + 2], padded[:, 1 : width + 3], padded[:, 2 : width + 4], courant_padded
    )
    return advect_step(
        first[:, :width], first[:, 1 : width + 1], first[:, 2 : width + 2], courant_padded[1:-1]
    )


def apply_root(multiply, vectors):
    root_coefs = chebyshev_root(0.5, 12.0)
    result = root_coefs[3] * vectors
    for degree in (2, 1, 0):
        result = multiply(result) + root_coefs[degree] * vectors
    return result


def network_kernel(x_ref, pred_ref, w_prof_ref, w_pred_ref, offset_ref, w_out_ref, w_phys_ref, out_ref):
    x = x_ref[...]
    narrow = x.astype(jnp.bfloat16)
    extra = pred_ref[...]
    total = jnp.dot(x, w_phys_ref[...], precision=highest, preferred_element_type=jnp.float32)
    for part in range(w_prof_ref.shape[0]):
        pre = jnp.dot(narrow, w_prof_ref[part], preferred_element_type=jnp.float32)
        pre = pre + jnp.dot(extra, w_pred_ref[part], preferred_element_type=jnp.float32)
        hidden = jnp.tanh(pre + offset_ref[...]).astype(jnp.bfloat16)
        total = total + jnp.dot(hidden, w_out_ref[part], preferred_element_type=jnp.float32)
    out_ref[...] = total


def block_diagonal(matrix, parts, dtype):
    eye = jnp.eye(parts, dtype=dtype)
    rows, cols = matrix.shape
    return (eye[:, :, None, None] * matrix.astype(dtype)[None, None]).reshape(parts, parts * rows, cols)


def network(packed, predictors, weighting, bias_in, bias_offset, bias_out, levels, rows=512):
    total_rows, lanes = packed.shape
    assert total_rows % rows == 0
    parts = lanes // levels
    hid = bias_in.shape[1]
    channels = bias_out.shape[1]
    npred = predictors.shape[1]
    w_prof = block_diagonal(bias_in[:levels], parts, jnp.bfloat16)
    w_pred = block_diagonal(bias_in[levels:], parts, jnp.bfloat16)
    out_parts = block_diagonal(bias_out.T, parts, jnp.bfloat16)
    w_out = jnp.transpose(out_parts.reshape(parts, parts, channels, hid), (0, 3, 1, 2)).reshape(
        parts, hid, parts * channels
    )
    phys_parts = block_diagonal(weighting.T, parts, jnp.float32)
    w_phys = jnp.transpose(phys_parts, (1, 0, 2)).reshape(parts * levels, parts * channels)
    column_groups = predictors.shape[0] // parts
    pred_tiled = jnp.tile(
        predictors.reshape(column_groups, parts * npred), (rows // column_groups, 1)
    )
    const = lambda i: (0, 0)
    const3 = lambda i: (0, 0, 0)
    return pl.pallas_call(
        network_kernel,
        out_shape=jax.ShapeDtypeStruct((total_rows, parts * channels), jnp.float32),
        grid=(total_rows // rows,),
        in_specs=[
            pl.BlockSpec((rows, lanes), lambda i: (i, 0)),
            pl.BlockSpec((rows, parts * npred), const),
            pl.BlockSpec((parts, lanes, hid), const3),
            pl.BlockSpec((parts, parts * npred, hid), const3),
            pl.BlockSpec((1, hid), const),
            pl.BlockSpec((parts, hid, parts * channels), const3),
            pl.BlockSpec((lanes, parts * channels), const),
        ],
        out_specs=pl.BlockSpec((rows, parts * channels), lambda i: (i, 0)),
        cost_estimate=pl.CostEstimate(
            flops=2 * total_rows * parts * hid * (lanes + parts * npred + parts * channels),
            transcendentals=total_rows * parts * hid,
            bytes_accessed=total_rows * (lanes + parts * channels) * 4,
        ),
    )(packed, pred_tiled, w_prof, w_pred, bias_offset.reshape(1, hid), w_out, w_phys)


def analyse(
    flat,
    predictors,
    obs_column,
    obs_channel,
    obs_value,
    weighting,
    bias_in,
    bias_offset,
    bias_out,
    obs_error,
    levels,
    columns,
):
    members = flat.shape[0]
    channels = weighting.shape[0]
    packed = flat.reshape(members * columns * levels // 128, 128)
    evolved = network(packed, predictors, weighting, bias_in, bias_offset, bias_out, levels)
    table = evolved.reshape(members, columns * channels)
    picks = obs_column * channels + obs_channel
    hx = jnp.take(table, picks, axis=1)
    onehot = (obs_channel[:, None] == jnp.arange(channels, dtype=jnp.int32)[None, :]).astype(
        jnp.float32
    )
    sigma = jnp.sum(onehot * obs_error[None, :], axis=1)
    hmean = jnp.mean(hx, axis=0)
    root_count = math.sqrt(members - 1)
    spread = ((hx - hmean) / (sigma * root_count)).astype(jnp.bfloat16)
    innov = (obs_value - hmean) / sigma
    spread_wide = spread.astype(jnp.float32)
    scale = 1.0 + jnp.sum(spread_wide * spread_wide) / members
    gram = jnp.dot(spread, spread.T, preferred_element_type=jnp.float32)
    mtx = (jnp.eye(members, dtype=jnp.float32) + gram) / scale

    def multiply_vector(vector):
        inner = jnp.sum(spread_wide * vector[:, None], axis=0)
        return (vector + jnp.sum(spread_wide * inner[None, :], axis=1)) / scale

    def multiply_fast(vectors):
        return jnp.dot(mtx, vectors, precision=lax.Precision.HIGH)

    drive = jnp.dot(spread_wide, innov, precision=highest)
    mean_weights = apply_root(multiply_vector, apply_root(multiply_vector, drive)) / (
        scale * root_count
    )
    xmean = jnp.mean(flat, axis=0)
    pert = flat - xmean
    spread_part = apply_root(multiply_fast, pert)
    shift_part = jnp.dot(mean_weights, pert, precision=highest)
    return xmean + spread_part / jnp.sqrt(scale) + shift_part


def shards(
    state,
    courant,
    weighting,
    bias_in,
    bias_offset,
    bias_out,
    predictors,
    obs_column,
    obs_channel,
    obs_value,
    obs_error,
):
    mem_local, levels, lon_local, lat_rows = state.shape
    groups = lax.axis_size("mem")
    patch_cols = lon_local * lat_rows // groups
    blocks = lat_rows // patch_cols
    field = jnp.transpose(state, (0, 2, 1, 3))
    wind = jnp.transpose(courant, (1, 0, 2))
    padded, wind_padded = exchange(field, wind)
    field = two_passes(padded, wind_padded)
    outgoing = field.reshape(mem_local, lon_local, levels, blocks, patch_cols)
    outgoing = jnp.transpose(outgoing, (1, 3, 0, 4, 2)).reshape(
        groups, mem_local, patch_cols * levels
    )
    arrived = lax.all_to_all(outgoing, "mem", split_axis=0, concat_axis=0, tiled=True)
    flat = arrived.reshape(groups * mem_local, patch_cols * levels)
    analysed = analyse(
        flat,
        predictors[0, 0],
        obs_column[0, 0],
        obs_channel[0, 0],
        obs_value[0, 0],
        weighting,
        bias_in,
        bias_offset,
        bias_out,
        obs_error,
        levels,
        patch_cols,
    )
    returning = analysed.reshape(groups, mem_local, patch_cols * levels)
    restored = lax.all_to_all(returning, "mem", split_axis=0, concat_axis=0, tiled=True)
    restored = restored.reshape(lon_local, blocks, mem_local, patch_cols, levels)
    restored = jnp.transpose(restored, (2, 0, 4, 1, 3)).reshape(
        mem_local, lon_local, levels, lat_rows
    )
    restored = with_layout_constraint(restored, Layout((0, 1, 2, 3)))
    padded, _ = exchange(restored)
    field = two_passes(padded, wind_padded)
    return jnp.transpose(field, (0, 2, 1, 3))


def solution(mesh):
    placed = (
        P("mem", None, "lon", None),
        P(None, "lon", None),
        P(),
        P(),
        P(),
        P(),
        P("mem", "lon", None, None),
        P("mem", "lon", None),
        P("mem", "lon", None),
        P("mem", "lon", None),
        P(),
    )
    return jax.shard_map(
        shards, mesh=mesh, in_specs=placed, out_specs=P("mem", None, "lon", None), check_vma=False
    )
```

```python
import functools
import math

import jax
import jax.numpy as jnp
from jax import lax
from jax.experimental import pallas as pl
from jax.experimental.layout import Layout, with_layout_constraint
from jax.experimental.pallas import tpu as pltpu
from jax.sharding import PartitionSpec as P

highest = lax.Precision.HIGHEST


def chebyshev_root(low_end, high_end):
    points = [
        0.5 * (high_end + low_end)
        + 0.5 * (high_end - low_end) * math.cos(math.pi * (index + 0.5) / 4.0)
        for index in range(4)
    ]
    coefficients = [0.0, 0.0, 0.0, 0.0]
    for index in range(4):
        basis_poly = [1.0]
        denominator = 1.0
        for other in range(4):
            if other != index:
                widened = [0.0] * (len(basis_poly) + 1)
                for power in range(len(basis_poly)):
                    widened[power + 1] += basis_poly[power]
                    widened[power] -= points[other] * basis_poly[power]
                basis_poly = widened
                denominator *= points[index] - points[other]
        factor = points[index] ** (-0.5) / denominator
        for power in range(4):
            coefficients[power] += factor * basis_poly[power]
    return tuple(coefficients)


def ring_shift(block, axis, step):
    count = lax.axis_size(axis)
    pairs = [(i, (i + step) % count) for i in range(count)]
    return lax.ppermute(block, axis, pairs)


def advect_step(west, centre, east, courant):
    return (
        centre
        - 0.5 * courant * (east - west)
        + 0.5 * courant * courant * (east - 2.0 * centre + west)
    )


def halo_padded(field, from_left, from_right):
    return jnp.concatenate([from_left, field, from_right], axis=1)


def exchange(field, wind=None):
    mem_local, width, levels, lat_rows = field.shape
    to_right = field[:, width - 2 :].reshape(mem_local * 2, levels, lat_rows)
    to_left = field[:, :2].reshape(mem_local * 2, levels, lat_rows)
    if wind is not None:
        to_right = jnp.concatenate([to_right, wind[-1:]], axis=0)
        to_left = jnp.concatenate([to_left, wind[:1]], axis=0)
    got_left = ring_shift(to_right, "lon", 1)
    got_right = ring_shift(to_left, "lon", -1)
    count = mem_local * 2
    padded = halo_padded(
        field,
        got_left[:count].reshape(mem_local, 2, levels, lat_rows),
        got_right[:count].reshape(mem_local, 2, levels, lat_rows),
    )
    if wind is None:
        return padded, None
    return padded, jnp.concatenate([got_left[count:], wind, got_right[count:]], axis=0)


def two_passes(padded, courant_padded):
    width = padded.shape[1] - 4
    first = advect_step(
        padded[:, : width + 2], padded[:, 1 : width + 3], padded[:, 2 : width + 4], courant_padded
    )
    return advect_step(
        first[:, :width], first[:, 1 : width + 1], first[:, 2 : width + 2], courant_padded[1:-1]
    )


def apply_root(multiply, vectors):
    root_coefs = chebyshev_root(0.5, 12.0)
    result = root_coefs[3] * vectors
    for degree in (2, 1, 0):
        result = multiply(result) + root_coefs[degree] * vectors
    return result


def network_kernel(x_ref, pred_ref, w_prof_ref, w_pred_ref, offset_ref, w_out_ref, w_phys_ref, out_ref):
    x = x_ref[...]
    narrow = x.astype(jnp.bfloat16)
    extra = pred_ref[...]
    total = jnp.dot(x, w_phys_ref[...], precision=highest, preferred_element_type=jnp.float32)
    for part in range(w_prof_ref.shape[0]):
        pre = jnp.dot(narrow, w_prof_ref[part], preferred_element_type=jnp.float32)
        pre = pre + jnp.dot(extra, w_pred_ref[part], preferred_element_type=jnp.float32)
        hidden = jnp.tanh(pre + offset_ref[...]).astype(jnp.bfloat16)
        total = total + jnp.dot(hidden, w_out_ref[part], preferred_element_type=jnp.float32)
    out_ref[...] = total


def block_diagonal(matrix, parts, dtype):
    eye = jnp.eye(parts, dtype=dtype)
    rows, cols = matrix.shape
    return (eye[:, :, None, None] * matrix.astype(dtype)[None, None]).reshape(parts, parts * rows, cols)


def network(packed, predictors, weighting, bias_in, bias_offset, bias_out, levels, rows=128):
    total_rows, lanes = packed.shape
    assert total_rows % rows == 0
    parts = lanes // levels
    hid = bias_in.shape[1]
    channels = bias_out.shape[1]
    npred = predictors.shape[1]
    w_prof = block_diagonal(bias_in[:levels], parts, jnp.bfloat16)
    w_pred = block_diagonal(bias_in[levels:], parts, jnp.bfloat16)
    out_parts = block_diagonal(bias_out.T, parts, jnp.bfloat16)
    w_out = jnp.transpose(out_parts.reshape(parts, parts, channels, hid), (0, 3, 1, 2)).reshape(
        parts, hid, parts * channels
    )
    phys_parts = block_diagonal(weighting.T, parts, jnp.float32)
    w_phys = jnp.transpose(phys_parts, (1, 0, 2)).reshape(parts * levels, parts * channels)
    column_groups = predictors.shape[0] // parts
    pred_tiled = jnp.tile(
        predictors.reshape(column_groups, parts * npred), (rows // column_groups, 1)
    )
    const = lambda i: (0, 0)
    const3 = lambda i: (0, 0, 0)
    return pl.pallas_call(
        network_kernel,
        out_shape=jax.ShapeDtypeStruct((total_rows, parts * channels), jnp.float32),
        grid=(total_rows // rows,),
        in_specs=[
            pl.BlockSpec((rows, lanes), lambda i: (i, 0)),
            pl.BlockSpec((rows, parts * npred), const),
            pl.BlockSpec((parts, lanes, hid), const3),
            pl.BlockSpec((parts, parts * npred, hid), const3),
            pl.BlockSpec((1, hid), const),
            pl.BlockSpec((parts, hid, parts * channels), const3),
            pl.BlockSpec((lanes, parts * channels), const),
        ],
        out_specs=pl.BlockSpec((rows, parts * channels), lambda i: (i, 0)),
        cost_estimate=pl.CostEstimate(
            flops=2 * total_rows * parts * hid * (lanes + parts * npred + parts * channels),
            transcendentals=total_rows * parts * hid,
            bytes_accessed=total_rows * (lanes + parts * channels) * 4,
        ),
    )(packed, pred_tiled, w_prof, w_pred, bias_offset.reshape(1, hid), w_out, w_phys)


def analyse(
    flat,
    predictors,
    obs_column,
    obs_channel,
    obs_value,
    weighting,
    bias_in,
    bias_offset,
    bias_out,
    obs_error,
    levels,
    columns,
):
    members = flat.shape[0]
    channels = weighting.shape[0]
    packed = flat.reshape(members * columns * levels // 128, 128)
    evolved = network(packed, predictors, weighting, bias_in, bias_offset, bias_out, levels)
    table = evolved.reshape(members, columns * channels)
    picks = obs_column * channels + obs_channel
    hx = jnp.take(table, picks, axis=1)
    onehot = (obs_channel[:, None] == jnp.arange(channels, dtype=jnp.int32)[None, :]).astype(
        jnp.float32
    )
    sigma = jnp.sum(onehot * obs_error[None, :], axis=1)
    hmean = jnp.mean(hx, axis=0)
    root_count = math.sqrt(members - 1)
    spread = ((hx - hmean) / (sigma * root_count)).astype(jnp.bfloat16)
    innov = (obs_value - hmean) / sigma
    spread_wide = spread.astype(jnp.float32)
    scale = 1.0 + jnp.sum(spread_wide * spread_wide) / members
    gram = jnp.dot(spread, spread.T, preferred_element_type=jnp.float32)
    mtx = (jnp.eye(members, dtype=jnp.float32) + gram) / scale

    def multiply_vector(vector):
        inner = jnp.sum(spread_wide * vector[:, None], axis=0)
        return (vector + jnp.sum(spread_wide * inner[None, :], axis=1)) / scale

    def multiply_fast(vectors):
        return jnp.dot(mtx, vectors, precision=lax.Precision.HIGH)

    drive = jnp.dot(spread_wide, innov, precision=highest)
    mean_weights = apply_root(multiply_vector, apply_root(multiply_vector, drive)) / (
        scale * root_count
    )
    xmean = jnp.mean(flat, axis=0)
    pert = flat - xmean
    spread_part = apply_root(multiply_fast, pert)
    shift_part = jnp.dot(mean_weights, pert, precision=highest)
    return xmean + spread_part / jnp.sqrt(scale) + shift_part


def shards(
    state,
    courant,
    weighting,
    bias_in,
    bias_offset,
    bias_out,
    predictors,
    obs_column,
    obs_channel,
    obs_value,
    obs_error,
):
    mem_local, levels, lon_local, lat_rows = state.shape
    groups = lax.axis_size("mem")
    patch_cols = lon_local * lat_rows // groups
    blocks = lat_rows // patch_cols
    field = jnp.transpose(state, (0, 2, 1, 3))
    wind = jnp.transpose(courant, (1, 0, 2))
    padded, wind_padded = exchange(field, wind)
    field = two_passes(padded, wind_padded)
    outgoing = field.reshape(mem_local, lon_local, levels, blocks, patch_cols)
    outgoing = jnp.transpose(outgoing, (1, 3, 0, 4, 2)).reshape(
        groups, mem_local, patch_cols * levels
    )
    arrived = lax.all_to_all(outgoing, "mem", split_axis=0, concat_axis=0, tiled=True)
    flat = arrived.reshape(groups * mem_local, patch_cols * levels)
    analysed = analyse(
        flat,
        predictors[0, 0],
        obs_column[0, 0],
        obs_channel[0, 0],
        obs_value[0, 0],
        weighting,
        bias_in,
        bias_offset,
        bias_out,
        obs_error,
        levels,
        patch_cols,
    )
    returning = analysed.reshape(groups, mem_local, patch_cols * levels)
    restored = lax.all_to_all(returning, "mem", split_axis=0, concat_axis=0, tiled=True)
    restored = restored.reshape(lon_local, blocks, mem_local, patch_cols, levels)
    restored = jnp.transpose(restored, (2, 0, 4, 1, 3)).reshape(
        mem_local, lon_local, levels, lat_rows
    )
    restored = with_layout_constraint(restored, Layout((0, 1, 2, 3)))
    padded, _ = exchange(restored)
    field = two_passes(padded, wind_padded)
    return jnp.transpose(field, (0, 2, 1, 3))


def solution(mesh):
    placed = (
        P("mem", None, "lon", None),
        P(None, "lon", None),
        P(),
        P(),
        P(),
        P(),
        P("mem", "lon", None, None),
        P("mem", "lon", None),
        P("mem", "lon", None),
        P("mem", "lon", None),
        P(),
    )
    return jax.shard_map(
        shards, mesh=mesh, in_specs=placed, out_specs=P("mem", None, "lon", None), check_vma=False
    )
```

```python
import functools
import math

import jax
import jax.numpy as jnp
from jax import lax
from jax.experimental import pallas as pl
from jax.experimental.layout import Layout, with_layout_constraint
from jax.experimental.pallas import tpu as pltpu
from jax.sharding import PartitionSpec as P

highest = lax.Precision.HIGHEST


def chebyshev_root(low_end, high_end):
    points = [
        0.5 * (high_end + low_end)
        + 0.5 * (high_end - low_end) * math.cos(math.pi * (index + 0.5) / 4.0)
        for index in range(4)
    ]
    coefficients = [0.0, 0.0, 0.0, 0.0]
    for index in range(4):
        basis_poly = [1.0]
        denominator = 1.0
        for other in range(4):
            if other != index:
                widened = [0.0] * (len(basis_poly) + 1)
                for power in range(len(basis_poly)):
                    widened[power + 1] += basis_poly[power]
                    widened[power] -= points[other] * basis_poly[power]
                basis_poly = widened
                denominator *= points[index] - points[other]
        factor = points[index] ** (-0.5) / denominator
        for power in range(4):
            coefficients[power] += factor * basis_poly[power]
    return tuple(coefficients)


def ring_shift(block, axis, step):
    count = lax.axis_size(axis)
    pairs = [(i, (i + step) % count) for i in range(count)]
    return lax.ppermute(block, axis, pairs)


def advect_step(west, centre, east, courant):
    return (
        centre
        - 0.5 * courant * (east - west)
        + 0.5 * courant * courant * (east - 2.0 * centre + west)
    )


def halo_padded(field, from_left, from_right):
    return jnp.concatenate([from_left, field, from_right], axis=1)


def exchange(field, wind=None):
    mem_local, width, levels, lat_rows = field.shape
    to_right = field[:, width - 2 :].reshape(mem_local * 2, levels, lat_rows)
    to_left = field[:, :2].reshape(mem_local * 2, levels, lat_rows)
    if wind is not None:
        to_right = jnp.concatenate([to_right, wind[-1:]], axis=0)
        to_left = jnp.concatenate([to_left, wind[:1]], axis=0)
    got_left = ring_shift(to_right, "lon", 1)
    got_right = ring_shift(to_left, "lon", -1)
    count = mem_local * 2
    padded = halo_padded(
        field,
        got_left[:count].reshape(mem_local, 2, levels, lat_rows),
        got_right[:count].reshape(mem_local, 2, levels, lat_rows),
    )
    if wind is None:
        return padded, None
    return padded, jnp.concatenate([got_left[count:], wind, got_right[count:]], axis=0)


def two_passes(padded, courant_padded):
    width = padded.shape[1] - 4
    first = advect_step(
        padded[:, : width + 2], padded[:, 1 : width + 3], padded[:, 2 : width + 4], courant_padded
    )
    return advect_step(
        first[:, :width], first[:, 1 : width + 1], first[:, 2 : width + 2], courant_padded[1:-1]
    )


def apply_root(multiply, vectors):
    root_coefs = chebyshev_root(0.5, 12.0)
    result = root_coefs[3] * vectors
    for degree in (2, 1, 0):
        result = multiply(result) + root_coefs[degree] * vectors
    return result


def network_kernel(
    x_ref, pred_ref, w_prof_ref, w_pred_ref, offset_ref, w_out_ref, w_phys_ref, out_ref, staged_ref
):
    x = x_ref[...]
    narrow = x.astype(jnp.bfloat16)
    extra = pred_ref[...]
    total = jnp.dot(x, w_phys_ref[...], precision=highest, preferred_element_type=jnp.float32)
    for part in range(w_prof_ref.shape[0]):
        pre = jnp.dot(narrow, w_prof_ref[part], preferred_element_type=jnp.float32)
        pre = pre + jnp.dot(extra, w_pred_ref[part], preferred_element_type=jnp.float32)
        hidden = jnp.tanh(pre + offset_ref[...]).astype(jnp.bfloat16)
        total = total + jnp.dot(hidden, w_out_ref[part], preferred_element_type=jnp.float32)
    rows, lanes = total.shape
    groups = out_ref.shape[1] // lanes
    staged_ref[...] = total
    for group in range(groups):
        out_ref[:, group * lanes : (group + 1) * lanes] = staged_ref[
            pl.ds(group, rows // groups, stride=groups), :
        ]


def block_diagonal(matrix, parts, dtype):
    eye = jnp.eye(parts, dtype=dtype)
    rows, cols = matrix.shape
    return (eye[:, :, None, None] * matrix.astype(dtype)[None, None]).reshape(parts, parts * rows, cols)


def network(packed, predictors, weighting, bias_in, bias_offset, bias_out, levels, rows=256):
    total_rows, lanes = packed.shape
    assert total_rows % rows == 0
    parts = lanes // levels
    hid = bias_in.shape[1]
    channels = bias_out.shape[1]
    npred = predictors.shape[1]
    w_prof = block_diagonal(bias_in[:levels], parts, jnp.bfloat16)
    w_pred = block_diagonal(bias_in[levels:], parts, jnp.bfloat16)
    out_parts = block_diagonal(bias_out.T, parts, jnp.bfloat16)
    w_out = jnp.transpose(out_parts.reshape(parts, parts, channels, hid), (0, 3, 1, 2)).reshape(
        parts, hid, parts * channels
    )
    phys_parts = block_diagonal(weighting.T, parts, jnp.float32)
    w_phys = jnp.transpose(phys_parts, (1, 0, 2)).reshape(parts * levels, parts * channels)
    column_groups = predictors.shape[0] // parts
    pred_tiled = jnp.tile(
        predictors.reshape(column_groups, parts * npred), (rows // column_groups, 1)
    )
    const = lambda i: (0, 0)
    const3 = lambda i: (0, 0, 0)
    return pl.pallas_call(
        network_kernel,
        out_shape=jax.ShapeDtypeStruct(
            (total_rows // column_groups, column_groups * parts * channels), jnp.float32
        ),
        grid=(total_rows // rows,),
        in_specs=[
            pl.BlockSpec((rows, lanes), lambda i: (i, 0)),
            pl.BlockSpec((rows, parts * npred), const),
            pl.BlockSpec((parts, lanes, hid), const3),
            pl.BlockSpec((parts, parts * npred, hid), const3),
            pl.BlockSpec((1, hid), const),
            pl.BlockSpec((parts, hid, parts * channels), const3),
            pl.BlockSpec((lanes, parts * channels), const),
        ],
        out_specs=pl.BlockSpec(
            (rows // column_groups, column_groups * parts * channels), lambda i: (i, 0)
        ),
        scratch_shapes=[pltpu.VMEM((rows, parts * channels), jnp.float32)],
        cost_estimate=pl.CostEstimate(
            flops=2 * total_rows * parts * hid * (lanes + parts * npred + parts * channels),
            transcendentals=total_rows * parts * hid,
            bytes_accessed=total_rows * (lanes + parts * channels) * 4,
        ),
    )(packed, pred_tiled, w_prof, w_pred, bias_offset.reshape(1, hid), w_out, w_phys)


def analyse(
    flat,
    predictors,
    obs_column,
    obs_channel,
    obs_value,
    weighting,
    bias_in,
    bias_offset,
    bias_out,
    obs_error,
    levels,
    columns,
):
    members = flat.shape[0]
    channels = weighting.shape[0]
    packed = flat.reshape(members * columns * levels // 128, 128)
    evolved = network(packed, predictors, weighting, bias_in, bias_offset, bias_out, levels)
    table = evolved.reshape(members, columns * channels)
    picks = obs_column * channels + obs_channel
    hx = jnp.take(table, picks, axis=1)
    onehot = (obs_channel[:, None] == jnp.arange(channels, dtype=jnp.int32)[None, :]).astype(
        jnp.float32
    )
    sigma = jnp.sum(onehot * obs_error[None, :], axis=1)
    hmean = jnp.mean(hx, axis=0)
    root_count = math.sqrt(members - 1)
    spread = ((hx - hmean) / (sigma * root_count)).astype(jnp.bfloat16)
    innov = (obs_value - hmean) / sigma
    spread_wide = spread.astype(jnp.float32)
    scale = 1.0 + jnp.sum(spread_wide * spread_wide) / members
    gram = jnp.dot(spread, spread.T, preferred_element_type=jnp.float32)
    mtx = (jnp.eye(members, dtype=jnp.float32) + gram) / scale

    def multiply_vector(vector):
        inner = jnp.sum(spread_wide * vector[:, None], axis=0)
        return (vector + jnp.sum(spread_wide * inner[None, :], axis=1)) / scale

    def multiply_fast(vectors):
        return jnp.dot(mtx, vectors, precision=lax.Precision.HIGH)

    drive = jnp.dot(spread_wide, innov, precision=highest)
    mean_weights = apply_root(multiply_vector, apply_root(multiply_vector, drive)) / (
        scale * root_count
    )
    xmean = jnp.mean(flat, axis=0)
    pert = flat - xmean
    spread_part = apply_root(multiply_fast, pert)
    shift_part = jnp.dot(mean_weights, pert, precision=highest)
    return xmean + spread_part / jnp.sqrt(scale) + shift_part


def shards(
    state,
    courant,
    weighting,
    bias_in,
    bias_offset,
    bias_out,
    predictors,
    obs_column,
    obs_channel,
    obs_value,
    obs_error,
):
    mem_local, levels, lon_local, lat_rows = state.shape
    groups = lax.axis_size("mem")
    patch_cols = lon_local * lat_rows // groups
    blocks = lat_rows // patch_cols
    field = jnp.transpose(state, (0, 2, 1, 3))
    wind = jnp.transpose(courant, (1, 0, 2))
    padded, wind_padded = exchange(field, wind)
    field = two_passes(padded, wind_padded)
    outgoing = field.reshape(mem_local, lon_local, levels, blocks, patch_cols)
    outgoing = jnp.transpose(outgoing, (1, 3, 0, 4, 2)).reshape(
        groups, mem_local, patch_cols * levels
    )
    arrived = lax.all_to_all(outgoing, "mem", split_axis=0, concat_axis=0, tiled=True)
    flat = arrived.reshape(groups * mem_local, patch_cols * levels)
    analysed = analyse(
        flat,
        predictors[0, 0],
        obs_column[0, 0],
        obs_channel[0, 0],
        obs_value[0, 0],
        weighting,
        bias_in,
        bias_offset,
        bias_out,
        obs_error,
        levels,
        patch_cols,
    )
    returning = analysed.reshape(groups, mem_local, patch_cols * levels)
    restored = lax.all_to_all(returning, "mem", split_axis=0, concat_axis=0, tiled=True)
    restored = restored.reshape(lon_local, blocks, mem_local, patch_cols, levels)
    restored = jnp.transpose(restored, (2, 0, 4, 1, 3)).reshape(
        mem_local, lon_local, levels, lat_rows
    )
    restored = with_layout_constraint(restored, Layout((0, 1, 2, 3)))
    padded, _ = exchange(restored)
    field = two_passes(padded, wind_padded)
    return jnp.transpose(field, (0, 2, 1, 3))


def solution(mesh):
    placed = (
        P("mem", None, "lon", None),
        P(None, "lon", None),
        P(),
        P(),
        P(),
        P(),
        P("mem", "lon", None, None),
        P("mem", "lon", None),
        P("mem", "lon", None),
        P("mem", "lon", None),
        P(),
    )
    return jax.shard_map(
        shards, mesh=mesh, in_specs=placed, out_specs=P("mem", None, "lon", None), check_vma=False
    )
```

```python
import functools
import math

import jax
import jax.numpy as jnp
from jax import lax
from jax.experimental import pallas as pl
from jax.experimental.layout import Layout, with_layout_constraint
from jax.experimental.pallas import tpu as pltpu
from jax.sharding import PartitionSpec as P

highest = lax.Precision.HIGHEST


def chebyshev_root(low_end, high_end):
    points = [
        0.5 * (high_end + low_end)
        + 0.5 * (high_end - low_end) * math.cos(math.pi * (index + 0.5) / 4.0)
        for index in range(4)
    ]
    coefficients = [0.0, 0.0, 0.0, 0.0]
    for index in range(4):
        basis_poly = [1.0]
        denominator = 1.0
        for other in range(4):
            if other != index:
                widened = [0.0] * (len(basis_poly) + 1)
                for power in range(len(basis_poly)):
                    widened[power + 1] += basis_poly[power]
                    widened[power] -= points[other] * basis_poly[power]
                basis_poly = widened
                denominator *= points[index] - points[other]
        factor = points[index] ** (-0.5) / denominator
        for power in range(4):
            coefficients[power] += factor * basis_poly[power]
    return tuple(coefficients)


def ring_shift(block, axis, step):
    count = lax.axis_size(axis)
    pairs = [(i, (i + step) % count) for i in range(count)]
    return lax.ppermute(block, axis, pairs)


def advect_step(west, centre, east, courant):
    return (
        centre
        - 0.5 * courant * (east - west)
        + 0.5 * courant * courant * (east - 2.0 * centre + west)
    )


def halo_padded(field, from_left, from_right):
    return jnp.concatenate([from_left, field, from_right], axis=1)


def exchange(field, wind=None):
    mem_local, width, levels, lat_rows = field.shape
    to_right = field[:, width - 2 :].reshape(mem_local * 2, levels, lat_rows)
    to_left = field[:, :2].reshape(mem_local * 2, levels, lat_rows)
    if wind is not None:
        to_right = jnp.concatenate([to_right, wind[-1:]], axis=0)
        to_left = jnp.concatenate([to_left, wind[:1]], axis=0)
    got_left = ring_shift(to_right, "lon", 1)
    got_right = ring_shift(to_left, "lon", -1)
    count = mem_local * 2
    padded = halo_padded(
        field,
        got_left[:count].reshape(mem_local, 2, levels, lat_rows),
        got_right[:count].reshape(mem_local, 2, levels, lat_rows),
    )
    if wind is None:
        return padded, None
    return padded, jnp.concatenate([got_left[count:], wind, got_right[count:]], axis=0)


def two_passes(padded, courant_padded):
    width = padded.shape[1] - 4
    first = advect_step(
        padded[:, : width + 2], padded[:, 1 : width + 3], padded[:, 2 : width + 4], courant_padded
    )
    return advect_step(
        first[:, :width], first[:, 1 : width + 1], first[:, 2 : width + 2], courant_padded[1:-1]
    )


def apply_root(multiply, vectors):
    root_coefs = chebyshev_root(0.5, 12.0)
    result = root_coefs[3] * vectors
    for degree in (2, 1, 0):
        result = multiply(result) + root_coefs[degree] * vectors
    return result


def network_kernel(
    x_ref, pred_ref, w_prof_ref, w_out_ref, w_phys_ref, out_ref, staged_ref
):
    x = x_ref[...]
    narrow = x.astype(jnp.bfloat16)
    extra = pred_ref[...]
    total = jnp.dot(x, w_phys_ref[...], precision=highest, preferred_element_type=jnp.float32)
    for part in range(w_prof_ref.shape[0]):
        pre = jnp.dot(narrow, w_prof_ref[part], preferred_element_type=jnp.float32)
        hidden = jnp.tanh(pre + extra[part]).astype(jnp.bfloat16)
        total = total + jnp.dot(hidden, w_out_ref[part], preferred_element_type=jnp.float32)
    rows, lanes = total.shape
    groups = out_ref.shape[1] // lanes
    staged_ref[...] = total
    for group in range(groups):
        out_ref[:, group * lanes : (group + 1) * lanes] = staged_ref[
            pl.ds(group, rows // groups, stride=groups), :
        ]


def block_diagonal(matrix, parts, dtype):
    eye = jnp.eye(parts, dtype=dtype)
    rows, cols = matrix.shape
    return (eye[:, :, None, None] * matrix.astype(dtype)[None, None]).reshape(parts, parts * rows, cols)


def network(packed, predictors, weighting, bias_in, bias_offset, bias_out, levels, rows=256):
    total_rows, lanes = packed.shape
    assert total_rows % rows == 0
    parts = lanes // levels
    hid = bias_in.shape[1]
    channels = bias_out.shape[1]
    npred = predictors.shape[1]
    w_prof = block_diagonal(bias_in[:levels], parts, jnp.bfloat16)
    out_parts = block_diagonal(bias_out.T, parts, jnp.bfloat16)
    w_out = jnp.transpose(out_parts.reshape(parts, parts, channels, hid), (0, 3, 1, 2)).reshape(
        parts, hid, parts * channels
    )
    phys_parts = block_diagonal(weighting.T, parts, jnp.float32)
    w_phys = jnp.transpose(phys_parts, (1, 0, 2)).reshape(parts * levels, parts * channels)
    column_groups = predictors.shape[0] // parts
    pred_term = jnp.dot(predictors, bias_in[levels:], preferred_element_type=jnp.float32)
    pred_term = (pred_term + bias_offset).reshape(column_groups, parts, hid)
    pred_tiled = jnp.tile(jnp.transpose(pred_term, (1, 0, 2)), (1, rows // column_groups, 1))
    const = lambda i: (0, 0)
    const3 = lambda i: (0, 0, 0)
    return pl.pallas_call(
        network_kernel,
        out_shape=jax.ShapeDtypeStruct(
            (total_rows // column_groups, column_groups * parts * channels), jnp.float32
        ),
        grid=(total_rows // rows,),
        in_specs=[
            pl.BlockSpec((rows, lanes), lambda i: (i, 0)),
            pl.BlockSpec((parts, rows, hid), const3),
            pl.BlockSpec((parts, lanes, hid), const3),
            pl.BlockSpec((parts, hid, parts * channels), const3),
            pl.BlockSpec((lanes, parts * channels), const),
        ],
        out_specs=pl.BlockSpec(
            (rows // column_groups, column_groups * parts * channels), lambda i: (i, 0)
        ),
        scratch_shapes=[pltpu.VMEM((rows, parts * channels), jnp.float32)],
        cost_estimate=pl.CostEstimate(
            flops=2 * total_rows * parts * hid * (lanes + parts * npred + parts * channels),
            transcendentals=total_rows * parts * hid,
            bytes_accessed=total_rows * (lanes + parts * channels) * 4,
        ),
    )(packed, pred_tiled, w_prof, w_out, w_phys)


def analyse(
    flat,
    predictors,
    obs_column,
    obs_channel,
    obs_value,
    weighting,
    bias_in,
    bias_offset,
    bias_out,
    obs_error,
    levels,
    columns,
):
    members = flat.shape[0]
    channels = weighting.shape[0]
    packed = flat.reshape(members * columns * levels // 128, 128)
    evolved = network(packed, predictors, weighting, bias_in, bias_offset, bias_out, levels)
    table = evolved.reshape(members, columns * channels)
    picks = obs_column * channels + obs_channel
    hx = jnp.take(table, picks, axis=1)
    onehot = (obs_channel[:, None] == jnp.arange(channels, dtype=jnp.int32)[None, :]).astype(
        jnp.float32
    )
    sigma = jnp.sum(onehot * obs_error[None, :], axis=1)
    hmean = jnp.mean(hx, axis=0)
    root_count = math.sqrt(members - 1)
    spread = ((hx - hmean) / (sigma * root_count)).astype(jnp.bfloat16)
    innov = (obs_value - hmean) / sigma
    spread_wide = spread.astype(jnp.float32)
    scale = 1.0 + jnp.sum(spread_wide * spread_wide) / members
    gram = jnp.dot(spread, spread.T, preferred_element_type=jnp.float32)
    mtx = (jnp.eye(members, dtype=jnp.float32) + gram) / scale

    def multiply_vector(vector):
        inner = jnp.sum(spread_wide * vector[:, None], axis=0)
        return (vector + jnp.sum(spread_wide * inner[None, :], axis=1)) / scale

    def multiply_fast(vectors):
        return jnp.dot(mtx, vectors, precision=lax.Precision.HIGH)

    drive = jnp.dot(spread_wide, innov, precision=highest)
    mean_weights = apply_root(multiply_vector, apply_root(multiply_vector, drive)) / (
        scale * root_count
    )
    xmean = jnp.mean(flat, axis=0)
    pert = flat - xmean
    spread_part = apply_root(multiply_fast, pert)
    shift_part = jnp.dot(mean_weights, pert, precision=highest)
    return xmean + spread_part / jnp.sqrt(scale) + shift_part


def shards(
    state,
    courant,
    weighting,
    bias_in,
    bias_offset,
    bias_out,
    predictors,
    obs_column,
    obs_channel,
    obs_value,
    obs_error,
):
    mem_local, levels, lon_local, lat_rows = state.shape
    groups = lax.axis_size("mem")
    patch_cols = lon_local * lat_rows // groups
    blocks = lat_rows // patch_cols
    field = jnp.transpose(state, (0, 2, 1, 3))
    wind = jnp.transpose(courant, (1, 0, 2))
    padded, wind_padded = exchange(field, wind)
    field = two_passes(padded, wind_padded)
    outgoing = field.reshape(mem_local, lon_local, levels, blocks, patch_cols)
    outgoing = jnp.transpose(outgoing, (1, 3, 0, 4, 2)).reshape(
        groups, mem_local, patch_cols * levels
    )
    arrived = lax.all_to_all(outgoing, "mem", split_axis=0, concat_axis=0, tiled=True)
    flat = arrived.reshape(groups * mem_local, patch_cols * levels)
    analysed = analyse(
        flat,
        predictors[0, 0],
        obs_column[0, 0],
        obs_channel[0, 0],
        obs_value[0, 0],
        weighting,
        bias_in,
        bias_offset,
        bias_out,
        obs_error,
        levels,
        patch_cols,
    )
    returning = analysed.reshape(groups, mem_local, patch_cols * levels)
    restored = lax.all_to_all(returning, "mem", split_axis=0, concat_axis=0, tiled=True)
    restored = restored.reshape(lon_local, blocks, mem_local, patch_cols, levels)
    restored = jnp.transpose(restored, (2, 0, 4, 1, 3)).reshape(
        mem_local, lon_local, levels, lat_rows
    )
    restored = with_layout_constraint(restored, Layout((0, 1, 2, 3)))
    padded, _ = exchange(restored)
    field = two_passes(padded, wind_padded)
    return jnp.transpose(field, (0, 2, 1, 3))


def solution(mesh):
    placed = (
        P("mem", None, "lon", None),
        P(None, "lon", None),
        P(),
        P(),
        P(),
        P(),
        P("mem", "lon", None, None),
        P("mem", "lon", None),
        P("mem", "lon", None),
        P("mem", "lon", None),
        P(),
    )
    return jax.shard_map(
        shards, mesh=mesh, in_specs=placed, out_specs=P("mem", None, "lon", None), check_vma=False
    )
```
